32 devices in a mesh: groups: 2 (over x), gx: 16 (over z, y, core).
Axes of the slice: x: 2, y: 2, z: 4, core: 2. Of those that a mesh axis runs over, the one named last changes fastest.
Arguments:
- voltages: bfloat16 [1024, 2, 8, 1024], P(('groups', 'gx')), parts along dimension 0, may hold values from -6 to 6
- history: float32 [1024, 126, 256], P(('groups', 'gx')), parts along dimension 0, may hold values from 0.25 to 4
- beam_pos: int32 [256, 2], replicated, may hold values from 0 to 63
- dm_list: int32 [1024], replicated, may hold values from 0 to 4095
- chan_map: int32 [512], P('gx'), may hold values from 0 to 511, each once
Outputs:
- spectrum_power: float32 [128, 1024, 256], P(('groups', 'gx')), parts along dimension 0
The draws below stay inside these ranges and needn't reach their ends.
There are 2 independent parts, one for each index of `groups`. The reference program is written for one: setup_inputs(seed, part) draws one part's arguments, and reference() takes and returns one part's arrays. A program takes and returns all parts, laid end to end along the dimension named above; an argument that names none is the same for every part. Nothing has to cross between parts.
Inputs may be any that keep to these rules, and one draw needn't show every extreme that they name: `chan_map`: each of 0 to 511 once.
All inputs are finite; a program needn't handle non-finite values.
Results may differ from the reference program's by a relative error of at most 0.0026.
Values may be sent and summed in bfloat16 or wider, within the bound.
No kernel may reach another device: no remote copies, remote signals or barrier semaphores. Data moves between devices by JAX's collectives and lax.ppermute only.
A program may use at most 64 MiB of HBM per device.

```python
import math
import jax
import jax.numpy as jnp
from jax import lax

ANTENNA_INPUTS = 1024
BEAMS = 256
DMS = 1024
HIST = 126
VOLTAGE_SAMPLES = 8
FREQ_CHANNELS = 512


def plant(values, own_key, low, top_value):
    extent = values.shape
    place = [jax.random.randint(jax.random.fold_in(own_key, axis), (), 0, extent[axis]) for axis in range(len(extent))]
    values = values.at[tuple(place)].set(low)
    longest = extent.index(max(extent))
    place[longest] = (place[longest] + 1) % extent[longest]
    return values.at[tuple(place)].set(top_value)


def block_scale(stream_key, shape, cuts, smallest, high):
    level = 1.0
    for position, parts in cuts:
        steps = jax.random.uniform(jax.random.fold_in(jax.random.fold_in(stream_key, 6), position), (parts,), jnp.float32, smallest / len(cuts), high / len(cuts))
        level = level * jnp.repeat(jnp.exp(steps), shape[position] // parts).reshape((-1,) + (1,) * (len(shape) - 1 - position))
    return level


def normal_values(key, extent, deviation, limit, split=(), held_as=jnp.bfloat16):
    drawn = jax.random.normal(key, extent, jnp.float32) * deviation
    if len(split) > 0:
        drawn = block_scale(key, extent, split, -0.22, 0.18) * drawn
    return jnp.clip(drawn, min=-limit, max=limit).astype(held_as)


def setup_inputs(seed: int = 0, part: int = 0) -> dict:
    streams_of = jax.random.split(jax.random.key(seed), 6)
    part_keys = jax.random.split(jax.random.fold_in(streams_of[5], part), 6)
    return {
        "voltages": normal_values(part_keys[0], (FREQ_CHANNELS, 2, VOLTAGE_SAMPLES, ANTENNA_INPUTS), 1.0, 6.0, ((0, 16),)),
        "history": jnp.clip(jnp.exp(math.log(4.0) - 2.7725887 * jax.random.uniform(part_keys[1], (FREQ_CHANNELS, HIST, BEAMS), jnp.float32) ** block_scale(part_keys[1], (FREQ_CHANNELS, HIST, BEAMS), ((0, 16),), -0.2, 0.2)), 0.25, 4.0),
        "beam_pos": plant(jax.random.randint(streams_of[2], (BEAMS, 2), 0, 64), jax.random.fold_in(streams_of[2], 1), 0, 63).astype(jnp.int32),
        "dm_list": plant(jax.random.randint(streams_of[3], (DMS,), 0, 4096), jax.random.fold_in(streams_of[3], 1), 0, 4095).astype(jnp.int32),
        "chan_map": jax.random.permutation(streams_of[4], FREQ_CHANNELS).astype(jnp.int32),
    }


def steering(freq_index, beam_pos, antennas):
    antenna_input = jnp.arange(antennas, dtype=jnp.int32)
    east_offset = antenna_input % 32
    north_pos = antenna_input // 32
    projection = east_offset[:, None] * beam_pos[None, :, 0] + north_pos[:, None] * beam_pos[None, :, 1]
    phase_step = freq_index[:, None, None] * projection[None, :, :] % 8192
    angles = phase_step.astype(jnp.float32) * (2.0 * math.pi / 8192.0)
    weight_scale = 1.0 / math.sqrt(antennas)
    return ((jnp.cos(angles) * weight_scale).astype(jnp.bfloat16), (jnp.sin(angles) * weight_scale).astype(jnp.bfloat16))

def detect_block(volt_block, cos_w, sin_w):
    highest = lax.Precision.HIGHEST
    cosine_term = jnp.einsum('cpsa,cab->cpsb', volt_block.astype(jnp.float32), cos_w.astype(jnp.float32), precision=highest)
    sin_part = jnp.einsum('cpsa,cab->cpsb', volt_block.astype(jnp.float32), sin_w.astype(jnp.float32), precision=highest)
    real_part = cosine_term[:, 0] + sin_part[:, 1]
    imag_part = cosine_term[:, 1] - sin_part[:, 0]
    power_now = real_part * real_part + imag_part * imag_part
    n_chan, n_samp, n_beam = power_now.shape
    return lax.optimization_barrier(jnp.mean(power_now.reshape(n_chan, n_samp // 4, 4, n_beam), axis=2))

def dft_table(bins):
    sample = jnp.arange(bins, dtype=jnp.int32)
    harmonic = jnp.arange(bins // 2, dtype=jnp.int32) + 1
    turn_count = sample[:, None] * harmonic[None, :] % bins
    angles = turn_count.astype(jnp.float32) * (2.0 * math.pi / bins)
    norm_scale = 1.0 / math.sqrt(bins)
    return jnp.concatenate([jnp.cos(angles) * norm_scale, -jnp.sin(angles) * norm_scale], axis=1)

def channel_lags(chan_map, channel_count):
    freq_index = 2 * channel_count - chan_map
    top_square = 2 * channel_count * (2 * channel_count) * 64
    return top_square // (freq_index * freq_index) - 64

def stacked_table(freq_number, lag, dm_list, bins):
    delay = dm_list[:, None] * lag[None, :] // 4096
    turn_count = (freq_number + 1) * delay % bins
    angles = turn_count.astype(jnp.float32) * (2.0 * math.pi / bins)
    cos_t = jnp.cos(angles).astype(jnp.bfloat16)
    sin_t = jnp.sin(angles).astype(jnp.bfloat16)
    upper = jnp.concatenate([cos_t, -sin_t], axis=1)
    lower = jnp.concatenate([sin_t, cos_t], axis=1)
    return jnp.concatenate([upper, lower], axis=0)

def reference(voltages, history, beam_pos, dm_list, chan_map):
    highest = lax.Precision.HIGHEST
    channel_count = chan_map.shape[0]
    block_size = math.gcd(channel_count, 8)
    samples = voltages.shape[2]
    antennas = voltages.shape[3]
    beams = beam_pos.shape[0]
    trials = dm_list.shape[0]
    volt_blocks = voltages.reshape(channel_count // block_size, block_size, 2, samples, antennas)
    freq_blocks = (2 * channel_count - chan_map).reshape(channel_count // block_size, block_size)

    def form_block(pair_args):
        volt_block, freq_block = pair_args
        cos_w, sin_w = steering(freq_block, beam_pos, antennas)
        return detect_block(volt_block, cos_w, sin_w)
    fresh_bins = lax.map(form_block, (volt_blocks, freq_blocks)).reshape(channel_count, samples // 4, beams)
    window = jnp.concatenate([history, fresh_bins], axis=1)
    bins = window.shape[1]
    freqs = bins // 2
    scaled = window / (lax.optimization_barrier(jnp.mean(window, axis=1, keepdims=True)) + 1e-06)
    spectra = jnp.einsum('ctb,tk->ckb', scaled, dft_table(bins), precision=highest).astype(jnp.bfloat16)
    spectra = spectra.reshape(channel_count, 2, freqs, beams)
    moved = jnp.moveaxis(spectra, 2, 0)
    lags = channel_lags(chan_map, channel_count)

    def search_freq(pair_args):
        freq_number, spec = pair_args
        table = stacked_table(freq_number, lags, dm_list, bins)
        right_side = jnp.transpose(spec, (1, 0, 2)).reshape(2 * channel_count, beams)
        out = jnp.dot(table, right_side, preferred_element_type=jnp.float32)
        real_out = out[:trials]
        imag_out = out[trials:]
        return (real_out * real_out + imag_out * imag_out) / channel_count
    return lax.map(search_freq, (jnp.arange(freqs, dtype=jnp.int32), moved))
```

```python
from functools import partial
import math

import jax
import jax.numpy as jnp
from jax import lax
from jax.experimental import pallas as pl
from jax.experimental.pallas import tpu as pltpu
from jax.sharding import PartitionSpec as P

GRID = 32
PHASES = 8192


def axis_tables(nu, pos, scale):
    idx = jnp.arange(GRID, dtype=jnp.int32)
    turns = (nu[:, None, None] * idx[None, :, None] * pos[None, None, :]) % PHASES
    angles = turns.astype(jnp.float32) * (2.0 * math.pi / PHASES)
    return jnp.cos(angles) * scale, jnp.sin(angles) * scale


def steering(nu, beam_pos, antennas):
    weight_scale = 1.0 / math.sqrt(antennas)
    ca, sa = axis_tables(nu, beam_pos[:, 0], weight_scale)
    cb, sb = axis_tables(nu, beam_pos[:, 1], 1.0)
    n_chan, _, beams = ca.shape
    w_cos = ca[:, None, :, :] * cb[:, :, None, :] - sa[:, None, :, :] * sb[:, :, None, :]
    w_sin = sa[:, None, :, :] * cb[:, :, None, :] + ca[:, None, :, :] * sb[:, :, None, :]
    w_cos = w_cos.reshape(n_chan, GRID * GRID, beams).astype(jnp.bfloat16)
    w_sin = w_sin.reshape(n_chan, GRID * GRID, beams).astype(jnp.bfloat16)
    return w_cos, w_sin


def dft_table(bins):
    sample = jnp.arange(bins, dtype=jnp.int32)
    harmonic = jnp.arange(bins // 2, dtype=jnp.int32) + 1
    turn_count = sample[:, None] * harmonic[None, :] % bins
    angles = turn_count.astype(jnp.float32) * (2.0 * math.pi / bins)
    norm_scale = 1.0 / math.sqrt(bins)
    both = jnp.stack([jnp.cos(angles) * norm_scale, -jnp.sin(angles) * norm_scale], axis=2)
    return both.reshape(bins, bins)


def channel_lags(chan_map, channel_count):
    freq_index = 2 * channel_count - chan_map
    top_square = 2 * channel_count * (2 * channel_count) * 64
    return top_square // (freq_index * freq_index) - 64


def dedisp_kernel(kp1_ref, dm_ref, lag_ref, tab_ref, spec_ref, out_ref, cos_buf, sin_buf, *, bins, channels):
    i = pl.program_id(0)
    kp1 = kp1_ref[i]
    delay = (dm_ref[...] * lag_ref[...]) // 4096
    turns = (kp1 * (delay & (bins - 1))) & (bins - 1)
    rows = turns.shape[0]
    cos_t = jnp.broadcast_to(tab_ref[0:1, :], (rows, 128))
    sin_t = jnp.broadcast_to(tab_ref[1:2, :], (rows, 128))
    for c in range(turns.shape[1] // 128):
        idx = turns[:, c * 128:(c + 1) * 128]
        cos_buf[:, c * 128:(c + 1) * 128] = jnp.take_along_axis(cos_t, idx, axis=1).astype(jnp.bfloat16)
        sin_buf[:, c * 128:(c + 1) * 128] = jnp.take_along_axis(sin_t, idx, axis=1).astype(jnp.bfloat16)
    s_re = spec_ref[0, 0]
    s_im = spec_ref[0, 1]
    cmat = cos_buf[...]
    smat = sin_buf[...]
    f32 = jnp.float32
    ded_re = jnp.dot(cmat, s_re, preferred_element_type=f32) - jnp.dot(smat, s_im, preferred_element_type=f32)
    ded_im = jnp.dot(smat, s_re, preferred_element_type=f32) + jnp.dot(cmat, s_im, preferred_element_type=f32)
    out_ref[0] = (ded_re * ded_re + ded_im * ded_im) / channels


def dedisperse(kp1, dm_list, lags, spec, bins):
    n_freq, _, channels, beams = spec.shape
    trials = dm_list.shape[0]
    tile_d = 256
    sample = jnp.arange(128, dtype=jnp.int32) % bins
    angles = sample.astype(jnp.float32) * (2.0 * math.pi / bins)
    tab = jnp.zeros((8, 128), jnp.float32)
    tab = tab.at[0].set(jnp.cos(angles).astype(jnp.bfloat16).astype(jnp.float32))
    tab = tab.at[1].set(jnp.sin(angles).astype(jnp.bfloat16).astype(jnp.float32))
    dm_col = dm_list.reshape(trials, 1)
    lag_row = lags.reshape(1, channels)
    grid_spec = pltpu.PrefetchScalarGridSpec(
        num_scalar_prefetch=1,
        grid=(n_freq, trials // tile_d),
        in_specs=[
            pl.BlockSpec((tile_d, 1), lambda i, j, k: (j, 0)),
            pl.BlockSpec((1, channels), lambda i, j, k: (0, 0)),
            pl.BlockSpec((8, 128), lambda i, j, k: (0, 0)),
            pl.BlockSpec((1, 2, channels, beams), lambda i, j, k: (i, 0, 0, 0)),
        ],
        out_specs=pl.BlockSpec((1, tile_d, beams), lambda i, j, k: (i, j, 0)),
        scratch_shapes=[
            pltpu.VMEM((tile_d, channels), jnp.bfloat16),
            pltpu.VMEM((tile_d, channels), jnp.bfloat16),
        ],
    )
    flops = 8 * n_freq * trials * channels * beams
    cost = pl.CostEstimate(
        flops=flops,
        transcendentals=0,
        bytes_accessed=n_freq * (2 * channels * beams * 2 + trials * beams * 4),
    )
    return pl.pallas_call(
        partial(dedisp_kernel, bins=bins, channels=channels),
        out_shape=jax.ShapeDtypeStruct((n_freq, trials, beams), jnp.float32),
        grid_spec=grid_spec,
        cost_estimate=cost,
    )(kp1, dm_col, lag_row, tab, spec)


def local(voltages, history, beam_pos, dm_list, chan_map):
    highest = lax.Precision.HIGHEST
    all_chan = lax.all_gather(chan_map, "gx", axis=0, tiled=True)
    all_chan, voltages = lax.optimization_barrier((all_chan, voltages))
    channel_count = all_chan.shape[0]
    local_chan = voltages.shape[0]
    block_size = math.gcd(local_chan, 8)
    samples = voltages.shape[2]
    antennas = voltages.shape[3]
    beams = beam_pos.shape[0]
    volt_blocks = voltages.reshape(local_chan // block_size, block_size, 2, samples, antennas)
    freq_blocks = (2 * channel_count - chan_map).reshape(local_chan // block_size, block_size)

    def form_block(pair_args):
        volt_block, freq_block = pair_args
        cos_w, sin_w = steering(freq_block, beam_pos, antennas)
        cosine_term = jnp.einsum(
            "cpsa,cab->cpsb", volt_block, cos_w, preferred_element_type=jnp.float32
        )
        sin_part = jnp.einsum(
            "cpsa,cab->cpsb", volt_block, sin_w, preferred_element_type=jnp.float32
        )
        real_part = cosine_term[:, 0] + sin_part[:, 1]
        imag_part = cosine_term[:, 1] - sin_part[:, 0]
        power_now = real_part * real_part + imag_part * imag_part
        return jnp.mean(power_now.reshape(block_size, samples // 4, 4, beams), axis=2)

    fresh_bins = lax.map(form_block, (volt_blocks, freq_blocks)).reshape(
        local_chan, samples // 4, beams
    )
    window = jnp.concatenate([history, fresh_bins], axis=1)
    bins = window.shape[1]
    freqs = bins // 2
    scaled = window / (jnp.mean(window, axis=1, keepdims=True) + 1e-06)
    table = dft_table(bins)
    spectra = jnp.einsum("ctb,tj->jcb", scaled, table, precision=highest).astype(jnp.bfloat16)
    spectra = spectra.reshape(freqs, 2, local_chan, beams)
    turned = lax.all_to_all(spectra, "gx", split_axis=0, concat_axis=2, tiled=True)
    freq_dev = turned.shape[0]
    lags = channel_lags(all_chan, channel_count)
    kp1 = lax.axis_index("gx") * freq_dev + jnp.arange(freq_dev, dtype=jnp.int32) + 1
    return dedisperse(kp1, dm_list, lags, turned, bins)


def solution(mesh):
    in_specs = (
        P(("groups", "gx"), None, None, None),
        P(("groups", "gx"), None, None),
        P(),
        P(),
        P("gx"),
    )
    out_specs = P(("groups", "gx"), None, None)
    return jax.shard_map(local, mesh=mesh, in_specs=in_specs, out_specs=out_specs, check_vma=False)
```

```python
from functools import partial
import math

import jax
import jax.numpy as jnp
from jax import lax
from jax.experimental import pallas as pl
from jax.experimental.pallas import tpu as pltpu
from jax.sharding import PartitionSpec as P

GRID = 32
PHASES = 8192


def axis_tables(nu, pos, scale):
    idx = jnp.arange(GRID, dtype=jnp.int32)
    turns = (nu[:, None, None] * idx[None, :, None] * pos[None, None, :]) % PHASES
    angles = turns.astype(jnp.float32) * (2.0 * math.pi / PHASES)
    return jnp.cos(angles) * scale, jnp.sin(angles) * scale


def steering(nu, beam_pos, antennas):
    weight_scale = 1.0 / math.sqrt(antennas)
    ca, sa = axis_tables(nu, beam_pos[:, 0], weight_scale)
    cb, sb = axis_tables(nu, beam_pos[:, 1], 1.0)
    n_chan, _, beams = ca.shape
    w_cos = ca[:, None, :, :] * cb[:, :, None, :] - sa[:, None, :, :] * sb[:, :, None, :]
    w_sin = sa[:, None, :, :] * cb[:, :, None, :] + ca[:, None, :, :] * sb[:, :, None, :]
    w_cos = w_cos.reshape(n_chan, GRID * GRID, beams).astype(jnp.bfloat16)
    w_sin = w_sin.reshape(n_chan, GRID * GRID, beams).astype(jnp.bfloat16)
    return w_cos, w_sin


def dft_table(bins):
    sample = jnp.arange(bins, dtype=jnp.int32)
    harmonic = jnp.arange(bins // 2, dtype=jnp.int32) + 1
    turn_count = sample[:, None] * harmonic[None, :] % bins
    angles = turn_count.astype(jnp.float32) * (2.0 * math.pi / bins)
    norm_scale = 1.0 / math.sqrt(bins)
    both = jnp.stack([jnp.cos(angles) * norm_scale, -jnp.sin(angles) * norm_scale], axis=2)
    return both.reshape(bins, bins)


def channel_lags(chan_map, channel_count):
    freq_index = 2 * channel_count - chan_map
    top_square = 2 * channel_count * (2 * channel_count) * 64
    return top_square // (freq_index * freq_index) - 64


def dedisp_kernel(kp1_ref, dm_ref, lag_ref, tab_ref, spec_ref, out_ref, cos_buf, sin_buf, *, bins, channels):
    i = pl.program_id(0)
    kp1 = kp1_ref[i]
    delay = (dm_ref[...] * lag_ref[...]) // 4096
    turns = (kp1 * (delay & (bins - 1))) & (bins - 1)
    rows = turns.shape[0]
    cos_t = jnp.broadcast_to(tab_ref[0:1, :], (rows, 128))
    sin_t = jnp.broadcast_to(tab_ref[1:2, :], (rows, 128))
    for c in range(turns.shape[1] // 128):
        idx = turns[:, c * 128:(c + 1) * 128]
        cos_buf[:, c * 128:(c + 1) * 128] = jnp.take_along_axis(cos_t, idx, axis=1).astype(jnp.bfloat16)
        sin_buf[:, c * 128:(c + 1) * 128] = jnp.take_along_axis(sin_t, idx, axis=1).astype(jnp.bfloat16)
    s_re = spec_ref[0, 0]
    s_im = spec_ref[0, 1]
    cmat = cos_buf[...]
    smat = sin_buf[...]
    f32 = jnp.float32
    ded_re = jnp.dot(cmat, s_re, preferred_element_type=f32) - jnp.dot(smat, s_im, preferred_element_type=f32)
    ded_im = jnp.dot(smat, s_re, preferred_element_type=f32) + jnp.dot(cmat, s_im, preferred_element_type=f32)
    out_ref[0] = (ded_re * ded_re + ded_im * ded_im) / channels


def dedisperse(kp1, dm_list, lags, spec, bins):
    n_freq, _, channels, beams = spec.shape
    trials = dm_list.shape[0]
    tile_d = 256
    sample = jnp.arange(128, dtype=jnp.int32) % bins
    angles = sample.astype(jnp.float32) * (2.0 * math.pi / bins)
    tab = jnp.zeros((8, 128), jnp.float32)
    tab = tab.at[0].set(jnp.cos(angles).astype(jnp.bfloat16).astype(jnp.float32))
    tab = tab.at[1].set(jnp.sin(angles).astype(jnp.bfloat16).astype(jnp.float32))
    dm_col = dm_list.reshape(trials, 1)
    lag_row = lags.reshape(1, channels)
    grid_spec = pltpu.PrefetchScalarGridSpec(
        num_scalar_prefetch=1,
        grid=(n_freq, trials // tile_d),
        in_specs=[
            pl.BlockSpec((tile_d, 1), lambda i, j, k: (j, 0)),
            pl.BlockSpec((1, channels), lambda i, j, k: (0, 0)),
            pl.BlockSpec((8, 128), lambda i, j, k: (0, 0)),
            pl.BlockSpec((1, 2, channels, beams), lambda i, j, k: (i, 0, 0, 0)),
        ],
        out_specs=pl.BlockSpec((1, tile_d, beams), lambda i, j, k: (i, j, 0)),
        scratch_shapes=[
            pltpu.VMEM((tile_d, channels), jnp.bfloat16),
            pltpu.VMEM((tile_d, channels), jnp.bfloat16),
        ],
    )
    flops = 8 * n_freq * trials * channels * beams
    cost = pl.CostEstimate(
        flops=flops,
        transcendentals=0,
        bytes_accessed=n_freq * (2 * channels * beams * 2 + trials * beams * 4),
    )
    return pl.pallas_call(
        partial(dedisp_kernel, bins=bins, channels=channels),
        out_shape=jax.ShapeDtypeStruct((n_freq, trials, beams), jnp.float32),
        grid_spec=grid_spec,
        cost_estimate=cost,
    )(kp1, dm_col, lag_row, tab, spec)


def beamform(volt_block, nu, beam_pos):
    n_chan, _, samples, antennas = volt_block.shape
    beams = beam_pos.shape[0]
    cos_w, sin_w = steering(nu, beam_pos, antennas)
    cosine_term = jnp.einsum("cpsa,cab->cpsb", volt_block, cos_w, preferred_element_type=jnp.float32)
    sin_part = jnp.einsum("cpsa,cab->cpsb", volt_block, sin_w, preferred_element_type=jnp.float32)
    real_part = cosine_term[:, 0] + sin_part[:, 1]
    imag_part = cosine_term[:, 1] - sin_part[:, 0]
    power_now = real_part * real_part + imag_part * imag_part
    return jnp.mean(power_now.reshape(n_chan, samples // 4, 4, beams), axis=2)


def spectra_of(history, fresh_bins):
    highest = lax.Precision.HIGHEST
    window = jnp.concatenate([history, fresh_bins], axis=1)
    bins = window.shape[1]
    scaled = window / (jnp.mean(window, axis=1, keepdims=True) + 1e-06)
    spectra = jnp.einsum("ctb,tj->jcb", scaled, dft_table(bins), precision=highest).astype(jnp.bfloat16)
    return spectra.reshape(bins // 2, 2, history.shape[0], history.shape[2])


def local(voltages, history, beam_pos, dm_list, chan_map):
    devices = lax.axis_size("gx")
    copies = jnp.broadcast_to(chan_map[None, :], (devices, chan_map.shape[0]))
    all_chan = lax.all_to_all(copies, "gx", split_axis=0, concat_axis=0, tiled=True).reshape(-1)
    channel_count = all_chan.shape[0]
    local_chan = voltages.shape[0]
    block_size = math.gcd(local_chan, 8)
    n_blocks = local_chan // block_size
    bins = history.shape[1] + voltages.shape[2] // 4
    nu_local = 2 * channel_count - chan_map
    pieces = []
    for blk in range(n_blocks):
        part = slice(blk * block_size, (blk + 1) * block_size)
        fresh = beamform(voltages[part], nu_local[part], beam_pos)
        spectra = spectra_of(history[part], fresh)
        pieces.append(lax.all_to_all(spectra, "gx", split_axis=0, concat_axis=2, tiled=True))
    turned = jnp.concatenate(pieces, axis=2)
    freq_dev = turned.shape[0]
    lags = channel_lags(all_chan, channel_count)
    lags = lags.reshape(devices, n_blocks, block_size).transpose(1, 0, 2).reshape(channel_count)
    kp1 = lax.axis_index("gx") * freq_dev + jnp.arange(freq_dev, dtype=jnp.int32) + 1
    return dedisperse(kp1, dm_list, lags, turned, bins)


def solution(mesh):
    in_specs = (
        P(("groups", "gx"), None, None, None),
        P(("groups", "gx"), None, None),
        P(),
        P(),
        P("gx"),
    )
    out_specs = P(("groups", "gx"), None, None)
    return jax.shard_map(local, mesh=mesh, in_specs=in_specs, out_specs=out_specs, check_vma=False)
```

```python
from functools import partial
import math

import jax
import jax.numpy as jnp
from jax import lax
from jax.experimental import pallas as pl
from jax.experimental.pallas import tpu as pltpu
from jax.sharding import PartitionSpec as P

GRID = 32
PHASES = 8192


def axis_tables(nu, pos, scale):
    idx = jnp.arange(GRID, dtype=jnp.int32)
    turns = (nu[:, None, None] * idx[None, :, None] * pos[None, None, :]) % PHASES
    angles = turns.astype(jnp.float32) * (2.0 * math.pi / PHASES)
    return jnp.cos(angles) * scale, jnp.sin(angles) * scale


def steering(nu, beam_pos, antennas):
    weight_scale = 1.0 / math.sqrt(antennas)
    ca, sa = axis_tables(nu, beam_pos[:, 0], weight_scale)
    cb, sb = axis_tables(nu, beam_pos[:, 1], 1.0)
    n_chan, _, beams = ca.shape
    w_cos = ca[:, None, :, :] * cb[:, :, None, :] - sa[:, None, :, :] * sb[:, :, None, :]
    w_sin = sa[:, None, :, :] * cb[:, :, None, :] + ca[:, None, :, :] * sb[:, :, None, :]
    w_cos = w_cos.reshape(n_chan, GRID * GRID, beams).astype(jnp.bfloat16)
    w_sin = w_sin.reshape(n_chan, GRID * GRID, beams).astype(jnp.bfloat16)
    return w_cos, w_sin


def dft_table(bins):
    sample = jnp.arange(bins, dtype=jnp.int32)
    harmonic = jnp.arange(bins // 2, dtype=jnp.int32) + 1
    turn_count = sample[:, None] * harmonic[None, :] % bins
    angles = turn_count.astype(jnp.float32) * (2.0 * math.pi / bins)
    norm_scale = 1.0 / math.sqrt(bins)
    both = jnp.stack([jnp.cos(angles) * norm_scale, -jnp.sin(angles) * norm_scale], axis=2)
    return both.reshape(bins, bins)


def channel_lags(chan_map, channel_count):
    freq_index = 2 * channel_count - chan_map
    top_square = 2 * channel_count * (2 * channel_count) * 64
    return top_square // (freq_index * freq_index) - 64


def dedisp_kernel(kp1_ref, dm_ref, lag_ref, tab_ref, spec_ref, out_ref, cos_buf, sin_buf, *, bins, channels):
    i = pl.program_id(0)
    kp1 = kp1_ref[i]
    delay = (dm_ref[...] * lag_ref[...]) // 4096
    turns = (kp1 * (delay & (bins - 1))) & (bins - 1)
    rows = turns.shape[0]
    cos_t = jnp.broadcast_to(tab_ref[0:1, :], (rows, 128))
    sin_t = jnp.broadcast_to(tab_ref[1:2, :], (rows, 128))
    for c in range(turns.shape[1] // 128):
        idx = turns[:, c * 128:(c + 1) * 128]
        cos_buf[:, c * 128:(c + 1) * 128] = jnp.take_along_axis(cos_t, idx, axis=1).astype(jnp.bfloat16)
        sin_buf[:, c * 128:(c + 1) * 128] = jnp.take_along_axis(sin_t, idx, axis=1).astype(jnp.bfloat16)
    s_re = spec_ref[0, 0]
    s_im = spec_ref[0, 1]
    cmat = cos_buf[...]
    smat = sin_buf[...]
    f32 = jnp.float32
    ded_re = jnp.dot(cmat, s_re, preferred_element_type=f32) - jnp.dot(smat, s_im, preferred_element_type=f32)
    ded_im = jnp.dot(smat, s_re, preferred_element_type=f32) + jnp.dot(cmat, s_im, preferred_element_type=f32)
    out_ref[0] = (ded_re * ded_re + ded_im * ded_im) / channels


def dedisperse(kp1, dm_list, lags, spec, bins):
    n_freq, _, channels, beams = spec.shape
    trials = dm_list.shape[0]
    tile_d = 256
    sample = jnp.arange(128, dtype=jnp.int32) % bins
    angles = sample.astype(jnp.float32) * (2.0 * math.pi / bins)
    tab = jnp.zeros((8, 128), jnp.float32)
    tab = tab.at[0].set(jnp.cos(angles).astype(jnp.bfloat16).astype(jnp.float32))
    tab = tab.at[1].set(jnp.sin(angles).astype(jnp.bfloat16).astype(jnp.float32))
    dm_col = dm_list.reshape(trials, 1)
    lag_row = lags.reshape(1, channels)
    grid_spec = pltpu.PrefetchScalarGridSpec(
        num_scalar_prefetch=1,
        grid=(n_freq, trials // tile_d),
        in_specs=[
            pl.BlockSpec((tile_d, 1), lambda i, j, k: (j, 0)),
            pl.BlockSpec((1, channels), lambda i, j, k: (0, 0)),
            pl.BlockSpec((8, 128), lambda i, j, k: (0, 0)),
            pl.BlockSpec((1, 2, channels, beams), lambda i, j, k: (i, 0, 0, 0)),
        ],
        out_specs=pl.BlockSpec((1, tile_d, beams), lambda i, j, k: (i, j, 0)),
        scratch_shapes=[
            pltpu.VMEM((tile_d, channels), jnp.bfloat16),
            pltpu.VMEM((tile_d, channels), jnp.bfloat16),
        ],
    )
    flops = 8 * n_freq * trials * channels * beams
    cost = pl.CostEstimate(
        flops=flops,
        transcendentals=0,
        bytes_accessed=n_freq * (2 * channels * beams * 2 + trials * beams * 4),
    )
    return pl.pallas_call(
        partial(dedisp_kernel, bins=bins, channels=channels),
        out_shape=jax.ShapeDtypeStruct((n_freq, trials, beams), jnp.float32),
        grid_spec=grid_spec,
        cost_estimate=cost,
    )(kp1, dm_col, lag_row, tab, spec)


def beamform(volt_block, nu, beam_pos):
    n_chan, _, samples, antennas = volt_block.shape
    beams = beam_pos.shape[0]
    cos_w, sin_w = steering(nu, beam_pos, antennas)
    cosine_term = jnp.einsum("cpsa,cab->cpsb", volt_block, cos_w, preferred_element_type=jnp.float32)
    sin_part = jnp.einsum("cpsa,cab->cpsb", volt_block, sin_w, preferred_element_type=jnp.float32)
    real_part = cosine_term[:, 0] + sin_part[:, 1]
    imag_part = cosine_term[:, 1] - sin_part[:, 0]
    power_now = real_part * real_part + imag_part * imag_part
    return jnp.mean(power_now.reshape(n_chan, samples // 4, 4, beams), axis=2)


def spectra_of(history, fresh_bins):
    highest = lax.Precision.HIGHEST
    window = jnp.concatenate([history, fresh_bins], axis=1)
    bins = window.shape[1]
    scaled = window / (jnp.mean(window, axis=1, keepdims=True) + 1e-06)
    spectra = jnp.einsum("ctb,tj->jcb", scaled, dft_table(bins), precision=highest).astype(jnp.bfloat16)
    return spectra.reshape(bins // 2, 2, history.shape[0], history.shape[2])


def gather_ring(values, axis, devices):
    me = lax.axis_index(axis)
    pieces = [values]
    for shift in range(1, devices):
        perm = [(src, (src + shift) % devices) for src in range(devices)]
        pieces.append(lax.ppermute(values, axis, perm))
    stacked = jnp.stack(pieces)
    order = (me - jnp.arange(devices, dtype=jnp.int32)) % devices
    return jnp.take(stacked, order, axis=0).reshape(-1)


def local(voltages, history, beam_pos, dm_list, chan_map):
    devices = lax.axis_size("gx")
    all_chan = gather_ring(chan_map, "gx", devices)
    channel_count = all_chan.shape[0]
    local_chan = voltages.shape[0]
    block_size = math.gcd(local_chan, 8)
    n_blocks = local_chan // block_size
    volt_blocks = voltages.reshape(n_blocks, block_size, *voltages.shape[1:])
    freq_blocks = (2 * channel_count - chan_map).reshape(n_blocks, block_size)
    fresh_bins = lax.map(lambda pair: beamform(pair[0], pair[1], beam_pos), (volt_blocks, freq_blocks))
    fresh_bins = fresh_bins.reshape(local_chan, -1, beam_pos.shape[0])
    spectra = spectra_of(history, fresh_bins)
    bins = 2 * spectra.shape[0]
    turned = lax.all_to_all(spectra, "gx", split_axis=0, concat_axis=2, tiled=True)
    freq_dev = turned.shape[0]
    lags = channel_lags(all_chan, channel_count)
    kp1 = lax.axis_index("gx") * freq_dev + jnp.arange(freq_dev, dtype=jnp.int32) + 1
    return dedisperse(kp1, dm_list, lags, turned, bins)


def solution(mesh):
    in_specs = (
        P(("groups", "gx"), None, None, None),
        P(("groups", "gx"), None, None),
        P(),
        P(),
        P("gx"),
    )
    out_specs = P(("groups", "gx"), None, None)
    return jax.shard_map(local, mesh=mesh, in_specs=in_specs, out_specs=out_specs, check_vma=False)
```

```python
from functools import partial
import math

import jax
import jax.numpy as jnp
from jax import lax
from jax.experimental import pallas as pl
from jax.experimental.pallas import tpu as pltpu
from jax.sharding import PartitionSpec as P

GRID = 32
PHASES = 8192


def axis_tables(nu, pos, scale):
    idx = jnp.arange(GRID, dtype=jnp.int32)
    turns = (nu[:, None, None] * idx[None, :, None] * pos[None, None, :]) % PHASES
    angles = turns.astype(jnp.float32) * (2.0 * math.pi / PHASES)
    return jnp.cos(angles) * scale, jnp.sin(angles) * scale


def steering(nu, beam_pos, antennas):
    weight_scale = 1.0 / math.sqrt(antennas)
    ca, sa = axis_tables(nu, beam_pos[:, 0], weight_scale)
    cb, sb = axis_tables(nu, beam_pos[:, 1], 1.0)
    n_chan, _, beams = ca.shape
    w_cos = ca[:, None, :, :] * cb[:, :, None, :] - sa[:, None, :, :] * sb[:, :, None, :]
    w_sin = sa[:, None, :, :] * cb[:, :, None, :] + ca[:, None, :, :] * sb[:, :, None, :]
    w_cos = w_cos.reshape(n_chan, GRID * GRID, beams).astype(jnp.bfloat16)
    w_sin = w_sin.reshape(n_chan, GRID * GRID, beams).astype(jnp.bfloat16)
    return w_cos, w_sin


def dft_table(bins):
    sample = jnp.arange(bins, dtype=jnp.int32)
    harmonic = jnp.arange(bins // 2, dtype=jnp.int32) + 1
    turn_count = sample[:, None] * harmonic[None, :] % bins
    angles = turn_count.astype(jnp.float32) * (2.0 * math.pi / bins)
    norm_scale = 1.0 / math.sqrt(bins)
    both = jnp.stack([jnp.cos(angles) * norm_scale, -jnp.sin(angles) * norm_scale], axis=2)
    return both.reshape(bins, bins)


def channel_lags(chan_map, channel_count):
    freq_index = 2 * channel_count - chan_map
    top_square = 2 * channel_count * (2 * channel_count) * 64
    return top_square // (freq_index * freq_index) - 64


def dedisp_kernel(kp1_ref, dm_ref, lag_ref, tab_ref, spec_ref, out_ref, cos_buf, sin_buf, *, bins, channels):
    i = pl.program_id(0)
    kp1 = kp1_ref[i]
    delay = (dm_ref[...] * lag_ref[...]) // 4096
    turns = (kp1 * (delay & (bins - 1))) & (bins - 1)
    rows = turns.shape[0]
    cos_t = jnp.broadcast_to(tab_ref[0:1, :], (rows, 128))
    sin_t = jnp.broadcast_to(tab_ref[1:2, :], (rows, 128))
    for c in range(turns.shape[1] // 128):
        idx = turns[:, c * 128:(c + 1) * 128]
        cos_buf[:, c * 128:(c + 1) * 128] = jnp.take_along_axis(cos_t, idx, axis=1).astype(jnp.bfloat16)
        sin_buf[:, c * 128:(c + 1) * 128] = jnp.take_along_axis(sin_t, idx, axis=1).astype(jnp.bfloat16)
    s_re = spec_ref[0, 0]
    s_im = spec_ref[0, 1]
    cmat = cos_buf[...]
    smat = sin_buf[...]
    f32 = jnp.float32
    ded_re = jnp.dot(cmat, s_re, preferred_element_type=f32) - jnp.dot(smat, s_im, preferred_element_type=f32)
    ded_im = jnp.dot(smat, s_re, preferred_element_type=f32) + jnp.dot(cmat, s_im, preferred_element_type=f32)
    out_ref[0] = (ded_re * ded_re + ded_im * ded_im) / channels


def dedisperse(kp1, dm_list, lags, spec, bins):
    n_freq, _, channels, beams = spec.shape
    trials = dm_list.shape[0]
    tile_d = 256
    sample = jnp.arange(128, dtype=jnp.int32) % bins
    angles = sample.astype(jnp.float32) * (2.0 * math.pi / bins)
    tab = jnp.zeros((8, 128), jnp.float32)
    tab = tab.at[0].set(jnp.cos(angles).astype(jnp.bfloat16).astype(jnp.float32))
    tab = tab.at[1].set(jnp.sin(angles).astype(jnp.bfloat16).astype(jnp.float32))
    dm_col = dm_list.reshape(trials, 1)
    lag_row = lags.reshape(1, channels)
    grid_spec = pltpu.PrefetchScalarGridSpec(
        num_scalar_prefetch=1,
        grid=(n_freq, trials // tile_d),
        in_specs=[
            pl.BlockSpec((tile_d, 1), lambda i, j, k: (j, 0)),
            pl.BlockSpec((1, channels), lambda i, j, k: (0, 0)),
            pl.BlockSpec((8, 128), lambda i, j, k: (0, 0)),
            pl.BlockSpec((1, 2, channels, beams), lambda i, j, k: (i, 0, 0, 0)),
        ],
        out_specs=pl.BlockSpec((1, tile_d, beams), lambda i, j, k: (i, j, 0)),
        scratch_shapes=[
            pltpu.VMEM((tile_d, channels), jnp.bfloat16),
            pltpu.VMEM((tile_d, channels), jnp.bfloat16),
        ],
    )
    flops = 8 * n_freq * trials * channels * beams
    cost = pl.CostEstimate(
        flops=flops,
        transcendentals=0,
        bytes_accessed=n_freq * (2 * channels * beams * 2 + trials * beams * 4),
    )
    return pl.pallas_call(
        partial(dedisp_kernel, bins=bins, channels=channels),
        out_shape=jax.ShapeDtypeStruct((n_freq, trials, beams), jnp.float32),
        grid_spec=grid_spec,
        cost_estimate=cost,
    )(kp1, dm_col, lag_row, tab, spec)


def beamform(volt_block, nu, beam_pos):
    n_chan, _, samples, antennas = volt_block.shape
    beams = beam_pos.shape[0]
    cos_w, sin_w = steering(nu, beam_pos, antennas)
    cosine_term = jnp.einsum("cpsa,cab->cpsb", volt_block, cos_w, preferred_element_type=jnp.float32)
    sin_part = jnp.einsum("cpsa,cab->cpsb", volt_block, sin_w, preferred_element_type=jnp.float32)
    real_part = cosine_term[:, 0] + sin_part[:, 1]
    imag_part = cosine_term[:, 1] - sin_part[:, 0]
    power_now = real_part * real_part + imag_part * imag_part
    return jnp.mean(power_now.reshape(n_chan, samples // 4, 4, beams), axis=2)


def spectra_of(history, fresh_bins):
    highest = lax.Precision.HIGHEST
    window = jnp.concatenate([history, fresh_bins], axis=1)
    bins = window.shape[1]
    scaled = window / (jnp.mean(window, axis=1, keepdims=True) + 1e-06)
    spectra = jnp.einsum("ctb,tj->jcb", scaled, dft_table(bins), precision=highest).astype(jnp.bfloat16)
    return spectra.reshape(bins // 2, 2, history.shape[0], history.shape[2])


def ring_rounds(devices):
    shifts = []
    shift = 1
    while shift < devices:
        shifts.append(shift)
        shift *= 2
    return shifts


def ring_round(stacked, axis, devices, shift):
    perm = [(src, (src + shift) % devices) for src in range(devices)]
    return jnp.concatenate([stacked, lax.ppermute(stacked, axis, perm)], axis=0)


def ring_order(stacked, axis, devices):
    me = lax.axis_index(axis)
    order = (me - jnp.arange(devices, dtype=jnp.int32)) % devices
    return jnp.take(stacked, order, axis=0).reshape(-1)


def local(voltages, history, beam_pos, dm_list, chan_map):
    devices = lax.axis_size("gx")
    channel_count = devices * chan_map.shape[0]
    local_chan = voltages.shape[0]
    block_size = math.gcd(local_chan, 8)
    n_blocks = local_chan // block_size
    volt_blocks = voltages.reshape(n_blocks, block_size, *voltages.shape[1:])
    freq_blocks = (2 * channel_count - chan_map).reshape(n_blocks, block_size)
    assert devices & (devices - 1) == 0
    shifts = ring_rounds(devices)
    stacked = chan_map[None]
    fresh = []
    volt_next, freq_next = volt_blocks[0], freq_blocks[0]
    for i in range(n_blocks):
        block = beamform(volt_next, freq_next, beam_pos)
        later = min(i + 1, n_blocks - 1)
        volt_next, freq_next = volt_blocks[later], freq_blocks[later]
        if i < len(shifts):
            stacked = ring_round(stacked, "gx", devices, shifts[i])
            stacked, block, volt_next, freq_next = lax.optimization_barrier(
                (stacked, block, volt_next, freq_next)
            )
        fresh.append(block)
    for shift in shifts[n_blocks:]:
        stacked = ring_round(stacked, "gx", devices, shift)
    all_chan = ring_order(stacked, "gx", devices)
    fresh_bins = jnp.concatenate(fresh, axis=0)
    spectra = spectra_of(history, fresh_bins)
    bins = 2 * spectra.shape[0]
    turned = lax.all_to_all(spectra, "gx", split_axis=0, concat_axis=2, tiled=True)
    freq_dev = turned.shape[0]
    lags = channel_lags(all_chan, channel_count)
    kp1 = lax.axis_index("gx") * freq_dev + jnp.arange(freq_dev, dtype=jnp.int32) + 1
    return dedisperse(kp1, dm_list, lags, turned, bins)


def solution(mesh):
    in_specs = (
        P(("groups", "gx"), None, None, None),
        P(("groups", "gx"), None, None),
        P(),
        P(),
        P("gx"),
    )
    out_specs = P(("groups", "gx"), None, None)
    return jax.shard_map(local, mesh=mesh, in_specs=in_specs, out_specs=out_specs, check_vma=False)
```

```python
from functools import partial
import math

import jax
import jax.numpy as jnp
from jax import lax
from jax.experimental import pallas as pl
from jax.experimental.pallas import tpu as pltpu
from jax.sharding import PartitionSpec as P

GRID = 32
PHASES = 8192


def axis_tables(nu, pos, scale):
    idx = jnp.arange(GRID, dtype=jnp.int32)
    turns = (nu[:, None, None] * idx[None, :, None] * pos[None, None, :]) % PHASES
    angles = turns.astype(jnp.float32) * (2.0 * math.pi / PHASES)
    return jnp.cos(angles) * scale, jnp.sin(angles) * scale


def steering(nu, beam_pos, antennas):
    weight_scale = 1.0 / math.sqrt(antennas)
    ca, sa = axis_tables(nu, beam_pos[:, 0], weight_scale)
    cb, sb = axis_tables(nu, beam_pos[:, 1], 1.0)
    n_chan, _, beams = ca.shape
    w_cos = ca[:, None, :, :] * cb[:, :, None, :] - sa[:, None, :, :] * sb[:, :, None, :]
    w_sin = sa[:, None, :, :] * cb[:, :, None, :] + ca[:, None, :, :] * sb[:, :, None, :]
    w_cos = w_cos.reshape(n_chan, GRID * GRID, beams).astype(jnp.bfloat16)
    w_sin = w_sin.reshape(n_chan, GRID * GRID, beams).astype(jnp.bfloat16)
    return w_cos, w_sin


def dft_table(bins):
    sample = jnp.arange(bins, dtype=jnp.int32)
    harmonic = jnp.arange(bins // 2, dtype=jnp.int32) + 1
    turn_count = sample[:, None] * harmonic[None, :] % bins
    angles = turn_count.astype(jnp.float32) * (2.0 * math.pi / bins)
    norm_scale = 1.0 / math.sqrt(bins)
    both = jnp.stack([jnp.cos(angles) * norm_scale, -jnp.sin(angles) * norm_scale], axis=2)
    return both.reshape(bins, bins)


def channel_lags(chan_map, channel_count):
    freq_index = 2 * channel_count - chan_map
    top_square = 2 * channel_count * (2 * channel_count) * 64
    return top_square // (freq_index * freq_index) - 64


def dedisp_kernel(kp1_ref, dm_ref, lag_ref, tab_ref, spec_ref, out_ref, cos_buf, sin_buf, *, bins, channels):
    i = pl.program_id(0)
    kp1 = kp1_ref[i]
    delay = (dm_ref[...] * lag_ref[...]) // 4096
    turns = (kp1 * (delay & (bins - 1))) & (bins - 1)
    rows = turns.shape[0]
    cos_t = jnp.broadcast_to(tab_ref[0:1, :], (rows, 128))
    sin_t = jnp.broadcast_to(tab_ref[1:2, :], (rows, 128))
    for c in range(turns.shape[1] // 128):
        idx = turns[:, c * 128:(c + 1) * 128]
        cos_buf[:, c * 128:(c + 1) * 128] = jnp.take_along_axis(cos_t, idx, axis=1).astype(jnp.bfloat16)
        sin_buf[:, c * 128:(c + 1) * 128] = jnp.take_along_axis(sin_t, idx, axis=1).astype(jnp.bfloat16)
    s_re = spec_ref[0, 0]
    s_im = spec_ref[0, 1]
    cmat = cos_buf[...]
    smat = sin_buf[...]
    f32 = jnp.float32
    ded_re = jnp.dot(cmat, s_re, preferred_element_type=f32) - jnp.dot(smat, s_im, preferred_element_type=f32)
    ded_im = jnp.dot(smat, s_re, preferred_element_type=f32) + jnp.dot(cmat, s_im, preferred_element_type=f32)
    out_ref[0] = (ded_re * ded_re + ded_im * ded_im) / channels


def dedisperse(kp1, dm_list, lags, spec, bins):
    n_freq, _, channels, beams = spec.shape
    trials = dm_list.shape[0]
    tile_d = 256
    sample = jnp.arange(128, dtype=jnp.int32) % bins
    angles = sample.astype(jnp.float32) * (2.0 * math.pi / bins)
    tab = jnp.zeros((8, 128), jnp.float32)
    tab = tab.at[0].set(jnp.cos(angles).astype(jnp.bfloat16).astype(jnp.float32))
    tab = tab.at[1].set(jnp.sin(angles).astype(jnp.bfloat16).astype(jnp.float32))
    dm_col = dm_list.reshape(trials, 1)
    lag_row = lags.reshape(1, channels)
    grid_spec = pltpu.PrefetchScalarGridSpec(
        num_scalar_prefetch=1,
        grid=(n_freq, trials // tile_d),
        in_specs=[
            pl.BlockSpec((tile_d, 1), lambda i, j, k: (j, 0)),
            pl.BlockSpec((1, channels), lambda i, j, k: (0, 0)),
            pl.BlockSpec((8, 128), lambda i, j, k: (0, 0)),
            pl.BlockSpec((1, 2, channels, beams), lambda i, j, k: (i, 0, 0, 0)),
        ],
        out_specs=pl.BlockSpec((1, tile_d, beams), lambda i, j, k: (i, j, 0)),
        scratch_shapes=[
            pltpu.VMEM((tile_d, channels), jnp.bfloat16),
            pltpu.VMEM((tile_d, channels), jnp.bfloat16),
        ],
    )
    flops = 8 * n_freq * trials * channels * beams
    cost = pl.CostEstimate(
        flops=flops,
        transcendentals=0,
        bytes_accessed=n_freq * (2 * channels * beams * 2 + trials * beams * 4),
    )
    return pl.pallas_call(
        partial(dedisp_kernel, bins=bins, channels=channels),
        out_shape=jax.ShapeDtypeStruct((n_freq, trials, beams), jnp.float32),
        grid_spec=grid_spec,
        cost_estimate=cost,
    )(kp1, dm_col, lag_row, tab, spec)


def front_kernel(ca_ref, sa_ref, cb_ref, sb_ref, volt_ref, hist_ref, dft_ref, out_ref, wc_buf, ws_buf, win_buf):
    ca = ca_ref[0]
    sa = sa_ref[0]
    rows = ca.shape[0]
    for n in range(cb_ref.shape[1]):
        cb = cb_ref[0, n:n + 1, :]
        sb = sb_ref[0, n:n + 1, :]
        wc_buf[n * rows:(n + 1) * rows, :] = (ca * cb - sa * sb).astype(jnp.bfloat16)
        ws_buf[n * rows:(n + 1) * rows, :] = (sa * cb + ca * sb).astype(jnp.bfloat16)
    f32 = jnp.float32
    v_re = volt_ref[0, 0]
    v_im = volt_ref[0, 1]
    wc = wc_buf[...]
    ws = ws_buf[...]
    beam_re = jnp.dot(v_re, wc, preferred_element_type=f32) + jnp.dot(v_im, ws, preferred_element_type=f32)
    beam_im = jnp.dot(v_im, wc, preferred_element_type=f32) - jnp.dot(v_re, ws, preferred_element_type=f32)
    power = beam_re * beam_re + beam_im * beam_im
    hist_len = hist_ref.shape[1]
    win_buf[0:hist_len, :] = hist_ref[0]
    samples = power.shape[0]
    for j in range(samples // 4):
        win_buf[hist_len + j:hist_len + j + 1, :] = jnp.mean(power[4 * j:4 * j + 4], axis=0, keepdims=True)
    window = win_buf[...]
    scaled = window / (jnp.mean(window, axis=0, keepdims=True) + 1e-06)
    spec = jnp.dot(dft_ref[...], scaled, precision=lax.Precision.HIGHEST, preferred_element_type=f32)
    out_ref[0] = spec.astype(jnp.bfloat16)


def front(voltages, history, nu, beam_pos):
    n_chan, _, samples, antennas = voltages.shape
    beams = beam_pos.shape[0]
    hist_len = history.shape[1]
    bins = hist_len + samples // 4
    weight_scale = 1.0 / math.sqrt(antennas)
    ca, sa = axis_tables(nu, beam_pos[:, 0], weight_scale)
    cb, sb = axis_tables(nu, beam_pos[:, 1], 1.0)
    dft_t = dft_table(bins).T
    table_spec = pl.BlockSpec((1, GRID, beams), lambda c: (c, 0, 0))
    cost = pl.CostEstimate(
        flops=n_chan * (8 * samples * antennas * beams + 6 * 2 * bins * bins * beams),
        transcendentals=0,
        bytes_accessed=n_chan * (4 * GRID * beams * 4 + 2 * samples * antennas * 2 + hist_len * beams * 4 + bins * beams * 2),
    )
    return pl.pallas_call(
        front_kernel,
        out_shape=jax.ShapeDtypeStruct((n_chan, bins, beams), jnp.bfloat16),
        grid=(n_chan,),
        in_specs=[
            table_spec,
            table_spec,
            table_spec,
            table_spec,
            pl.BlockSpec((1, 2, samples, antennas), lambda c: (c, 0, 0, 0)),
            pl.BlockSpec((1, hist_len, beams), lambda c: (c, 0, 0)),
            pl.BlockSpec((bins, bins), lambda c: (0, 0)),
        ],
        out_specs=pl.BlockSpec((1, bins, beams), lambda c: (c, 0, 0)),
        scratch_shapes=[
            pltpu.VMEM((GRID * GRID, beams), jnp.bfloat16),
            pltpu.VMEM((GRID * GRID, beams), jnp.bfloat16),
            pltpu.VMEM((bins, beams), jnp.float32),
        ],
        cost_estimate=cost,
    )(ca, sa, cb, sb, voltages, history, dft_t)


def beamform(volt_block, nu, beam_pos):
    n_chan, _, samples, antennas = volt_block.shape
    beams = beam_pos.shape[0]
    cos_w, sin_w = steering(nu, beam_pos, antennas)
    cosine_term = jnp.einsum("cpsa,cab->cpsb", volt_block, cos_w, preferred_element_type=jnp.float32)
    sin_part = jnp.einsum("cpsa,cab->cpsb", volt_block, sin_w, preferred_element_type=jnp.float32)
    real_part = cosine_term[:, 0] + sin_part[:, 1]
    imag_part = cosine_term[:, 1] - sin_part[:, 0]
    power_now = real_part * real_part + imag_part * imag_part
    return jnp.mean(power_now.reshape(n_chan, samples // 4, 4, beams), axis=2)


def spectra_of(history, fresh_bins):
    highest = lax.Precision.HIGHEST
    window = jnp.concatenate([history, fresh_bins], axis=1)
    bins = window.shape[1]
    scaled = window / (jnp.mean(window, axis=1, keepdims=True) + 1e-06)
    spectra = jnp.einsum("ctb,tj->jcb", scaled, dft_table(bins), precision=highest).astype(jnp.bfloat16)
    return spectra.reshape(bins // 2, 2, history.shape[0], history.shape[2])


def ring_rounds(devices):
    shifts = []
    shift = 1
    while shift < devices:
        shifts.append(shift)
        shift *= 2
    return shifts


def ring_round(stacked, axis, devices, shift):
    perm = [(src, (src + shift) % devices) for src in range(devices)]
    return jnp.concatenate([stacked, lax.ppermute(stacked, axis, perm)], axis=0)


def ring_order(stacked, axis, devices):
    me = lax.axis_index(axis)
    order = (me - jnp.arange(devices, dtype=jnp.int32)) % devices
    return jnp.take(stacked, order, axis=0).reshape(-1)


def local(voltages, history, beam_pos, dm_list, chan_map):
    devices = lax.axis_size("gx")
    channel_count = devices * chan_map.shape[0]
    local_chan = voltages.shape[0]
    nu_local = 2 * channel_count - chan_map
    assert devices & (devices - 1) == 0
    stacked = chan_map[None]
    for shift in ring_rounds(devices):
        stacked = ring_round(stacked, "gx", devices, shift)
    all_chan = ring_order(stacked, "gx", devices)
    spec_c = front(voltages, history, nu_local, beam_pos)
    all_chan, spec_c = lax.optimization_barrier((all_chan, spec_c))
    bins = spec_c.shape[1]
    spectra = spec_c.transpose(1, 0, 2).reshape(bins // 2, 2, local_chan, spec_c.shape[2])
    turned = lax.all_to_all(spectra, "gx", split_axis=0, concat_axis=2, tiled=True)
    freq_dev = turned.shape[0]
    lags = channel_lags(all_chan, channel_count)
    kp1 = lax.axis_index("gx") * freq_dev + jnp.arange(freq_dev, dtype=jnp.int32) + 1
    return dedisperse(kp1, dm_list, lags, turned, bins)


def solution(mesh):
    in_specs = (
        P(("groups", "gx"), None, None, None),
        P(("groups", "gx"), None, None),
        P(),
        P(),
        P("gx"),
    )
    out_specs = P(("groups", "gx"), None, None)
    return jax.shard_map(local, mesh=mesh, in_specs=in_specs, out_specs=out_specs, check_vma=False)
```

```python
from functools import partial
import math

import jax
import jax.numpy as jnp
from jax import lax
from jax.experimental import pallas as pl
from jax.experimental.pallas import tpu as pltpu
from jax.sharding import PartitionSpec as P

GRID = 32
PHASES = 8192


def axis_tables(nu, pos, scale):
    step = (nu[:, None] * pos[None, :]) % PHASES

    def trig(mult, factor):
        turns = (step[:, None, :] * (mult[None, :, None] * factor)) % PHASES
        angles = turns.astype(jnp.float32) * (2.0 * math.pi / PHASES)
        return jnp.cos(angles), jnp.sin(angles)

    lo = jnp.arange(8, dtype=jnp.int32)
    hi = jnp.arange(GRID // 8, dtype=jnp.int32)
    c_lo, s_lo = trig(lo, 1)
    c_hi, s_hi = trig(hi, 8)
    cos_t = c_hi[:, :, None, :] * c_lo[:, None, :, :] - s_hi[:, :, None, :] * s_lo[:, None, :, :]
    sin_t = s_hi[:, :, None, :] * c_lo[:, None, :, :] + c_hi[:, :, None, :] * s_lo[:, None, :, :]
    shape = (nu.shape[0], GRID, pos.shape[0])
    return cos_t.reshape(shape) * scale, sin_t.reshape(shape) * scale


def steering(nu, beam_pos, antennas):
    weight_scale = 1.0 / math.sqrt(antennas)
    ca, sa = axis_tables(nu, beam_pos[:, 0], weight_scale)
    cb, sb = axis_tables(nu, beam_pos[:, 1], 1.0)
    n_chan, _, beams = ca.shape
    w_cos = ca[:, None, :, :] * cb[:, :, None, :] - sa[:, None, :, :] * sb[:, :, None, :]
    w_sin = sa[:, None, :, :] * cb[:, :, None, :] + ca[:, None, :, :] * sb[:, :, None, :]
    w_cos = w_cos.reshape(n_chan, GRID * GRID, beams).astype(jnp.bfloat16)
    w_sin = w_sin.reshape(n_chan, GRID * GRID, beams).astype(jnp.bfloat16)
    return w_cos, w_sin


def dft_table(bins):
    sample = jnp.arange(bins, dtype=jnp.int32)
    harmonic = jnp.arange(bins // 2, dtype=jnp.int32) + 1
    turn_count = sample[:, None] * harmonic[None, :] % bins
    angles = turn_count.astype(jnp.float32) * (2.0 * math.pi / bins)
    norm_scale = 1.0 / math.sqrt(bins)
    both = jnp.stack([jnp.cos(angles) * norm_scale, -jnp.sin(angles) * norm_scale], axis=2)
    return both.reshape(bins, bins)


def channel_lags(chan_map, channel_count):
    freq_index = 2 * channel_count - chan_map
    top_square = 2 * channel_count * (2 * channel_count) * 64
    return top_square // (freq_index * freq_index) - 64


def dedisp_kernel(resid_ref, tab_ref, spec_ref, out_ref, cos_buf, sin_buf, *, channels):
    rows = resid_ref.shape[0]
    cos_t = jnp.broadcast_to(tab_ref[0, 0:1, :], (rows, 128))
    sin_t = jnp.broadcast_to(tab_ref[0, 1:2, :], (rows, 128))
    for c in range(resid_ref.shape[1] // 128):
        idx = resid_ref[:, c * 128:(c + 1) * 128]
        cos_buf[:, c * 128:(c + 1) * 128] = jnp.take_along_axis(cos_t, idx, axis=1).astype(jnp.bfloat16)
        sin_buf[:, c * 128:(c + 1) * 128] = jnp.take_along_axis(sin_t, idx, axis=1).astype(jnp.bfloat16)
    s_re = spec_ref[0, 0]
    s_im = spec_ref[0, 1]
    cmat = cos_buf[...]
    smat = sin_buf[...]
    f32 = jnp.float32
    ded_re = jnp.dot(cmat, s_re, preferred_element_type=f32) - jnp.dot(smat, s_im, preferred_element_type=f32)
    ded_im = jnp.dot(smat, s_re, preferred_element_type=f32) + jnp.dot(cmat, s_im, preferred_element_type=f32)
    out_ref[0] = (ded_re * ded_re + ded_im * ded_im) / channels


def dedisperse(kp1, dm_list, lags, spec, bins):
    n_freq, _, channels, beams = spec.shape
    trials = dm_list.shape[0]
    tile_d = 256
    resid = ((dm_list[:, None] * lags[None, :]) // 4096) % bins
    sample = jnp.arange(128, dtype=jnp.int32) % bins
    turns = (kp1[:, None] * sample[None, :]) % bins
    angles = turns.astype(jnp.float32) * (2.0 * math.pi / bins)
    tab = jnp.zeros((n_freq, 8, 128), jnp.float32)
    tab = tab.at[:, 0].set(jnp.cos(angles).astype(jnp.bfloat16).astype(jnp.float32))
    tab = tab.at[:, 1].set(jnp.sin(angles).astype(jnp.bfloat16).astype(jnp.float32))
    flops = 8 * n_freq * trials * channels * beams
    cost = pl.CostEstimate(
        flops=flops,
        transcendentals=0,
        bytes_accessed=trials * channels * 4 + trials // tile_d * n_freq * 2 * channels * beams * 2
        + n_freq * trials * beams * 4,
    )
    return pl.pallas_call(
        partial(dedisp_kernel, channels=channels),
        out_shape=jax.ShapeDtypeStruct((n_freq, trials, beams), jnp.float32),
        grid=(trials // tile_d, n_freq),
        in_specs=[
            pl.BlockSpec((tile_d, channels), lambda j, i: (j, 0)),
            pl.BlockSpec((1, 8, 128), lambda j, i: (i, 0, 0)),
            pl.BlockSpec((1, 2, channels, beams), lambda j, i: (i, 0, 0, 0)),
        ],
        out_specs=pl.BlockSpec((1, tile_d, beams), lambda j, i: (i, j, 0)),
        scratch_shapes=[
            pltpu.VMEM((tile_d, channels), jnp.bfloat16),
            pltpu.VMEM((tile_d, channels), jnp.bfloat16),
        ],
        cost_estimate=cost,
    )(resid, tab, spec)


def beamform(volt_block, nu, beam_pos):
    n_chan, _, samples, antennas = volt_block.shape
    beams = beam_pos.shape[0]
    cos_w, sin_w = steering(nu, beam_pos, antennas)
    cosine_term = jnp.einsum("cpsa,cab->cpsb", volt_block, cos_w, preferred_element_type=jnp.float32)
    sin_part = jnp.einsum("cpsa,cab->cpsb", volt_block, sin_w, preferred_element_type=jnp.float32)
    real_part = cosine_term[:, 0] + sin_part[:, 1]
    imag_part = cosine_term[:, 1] - sin_part[:, 0]
    power_now = real_part * real_part + imag_part * imag_part
    return jnp.mean(power_now.reshape(n_chan, samples // 4, 4, beams), axis=2)


def spectra_of(history, fresh_bins):
    highest = lax.Precision.HIGHEST
    window = jnp.concatenate([history, fresh_bins], axis=1)
    bins = window.shape[1]
    scaled = window / (jnp.mean(window, axis=1, keepdims=True) + 1e-06)
    spectra = jnp.einsum("ctb,tj->jcb", scaled, dft_table(bins), precision=highest).astype(jnp.bfloat16)
    return spectra.reshape(bins // 2, 2, history.shape[0], history.shape[2])


def ring_rounds(devices):
    shifts = []
    shift = 1
    while shift < devices:
        shifts.append(shift)
        shift *= 2
    return shifts


def ring_round(stacked, axis, devices, shift):
    perm = [(src, (src + shift) % devices) for src in range(devices)]
    return jnp.concatenate([stacked, lax.ppermute(stacked, axis, perm)], axis=0)


def ring_order(stacked, axis, devices):
    me = lax.axis_index(axis)
    order = (me - jnp.arange(devices, dtype=jnp.int32)) % devices
    return jnp.take(stacked, order, axis=0).reshape(-1)


def local(voltages, history, beam_pos, dm_list, chan_map):
    devices = lax.axis_size("gx")
    channel_count = devices * chan_map.shape[0]
    local_chan = voltages.shape[0]
    block_size = math.gcd(local_chan, 8)
    n_blocks = local_chan // block_size
    volt_blocks = voltages.reshape(n_blocks, block_size, *voltages.shape[1:])
    freq_blocks = (2 * channel_count - chan_map).reshape(n_blocks, block_size)
    assert devices & (devices - 1) == 0
    shifts = ring_rounds(devices)
    stacked = chan_map[None]
    fresh = []
    volt_next, freq_next = volt_blocks[0], freq_blocks[0]
    for i in range(n_blocks):
        block = beamform(volt_next, freq_next, beam_pos)
        later = min(i + 1, n_blocks - 1)
        volt_next, freq_next = volt_blocks[later], freq_blocks[later]
        if i < len(shifts):
            stacked = ring_round(stacked, "gx", devices, shifts[i])
            stacked, block, volt_next, freq_next = lax.optimization_barrier(
                (stacked, block, volt_next, freq_next)
            )
        fresh.append(block)
    for shift in shifts[n_blocks:]:
        stacked = ring_round(stacked, "gx", devices, shift)
    all_chan = ring_order(stacked, "gx", devices)
    fresh_bins = jnp.concatenate(fresh, axis=0)
    spectra = spectra_of(history, fresh_bins)
    bins = 2 * spectra.shape[0]
    turned = lax.all_to_all(spectra, "gx", split_axis=0, concat_axis=2, tiled=True)
    freq_dev = turned.shape[0]
    lags = channel_lags(all_chan, channel_count)
    kp1 = lax.axis_index("gx") * freq_dev + jnp.arange(freq_dev, dtype=jnp.int32) + 1
    return dedisperse(kp1, dm_list, lags, turned, bins)


def solution(mesh):
    in_specs = (
        P(("groups", "gx"), None, None, None),
        P(("groups", "gx"), None, None),
        P(),
        P(),
        P("gx"),
    )
    out_specs = P(("groups", "gx"), None, None)
    return jax.shard_map(local, mesh=mesh, in_specs=in_specs, out_specs=out_specs, check_vma=False)
```

```python
from functools import partial
import math

import jax
import jax.numpy as jnp
from jax import lax
from jax.experimental import pallas as pl
from jax.experimental.pallas import tpu as pltpu
from jax.sharding import PartitionSpec as P

GRID = 32
PHASES = 8192


def axis_tables(nu, pos, scale):
    step = (nu[:, None] * pos[None, :]) % PHASES

    def trig(mult, factor):
        turns = (step[:, None, :] * (mult[None, :, None] * factor)) % PHASES
        angles = turns.astype(jnp.float32) * (2.0 * math.pi / PHASES)
        return jnp.cos(angles), jnp.sin(angles)

    lo = jnp.arange(8, dtype=jnp.int32)
    hi = jnp.arange(GRID // 8, dtype=jnp.int32)
    c_lo, s_lo = trig(lo, 1)
    c_hi, s_hi = trig(hi, 8)
    cos_t = c_hi[:, :, None, :] * c_lo[:, None, :, :] - s_hi[:, :, None, :] * s_lo[:, None, :, :]
    sin_t = s_hi[:, :, None, :] * c_lo[:, None, :, :] + c_hi[:, :, None, :] * s_lo[:, None, :, :]
    shape = (nu.shape[0], GRID, pos.shape[0])
    return cos_t.reshape(shape) * scale, sin_t.reshape(shape) * scale


def steering(nu, beam_pos, antennas):
    weight_scale = 1.0 / math.sqrt(antennas)
    ca, sa = axis_tables(nu, beam_pos[:, 0], weight_scale)
    cb, sb = axis_tables(nu, beam_pos[:, 1], 1.0)
    n_chan, _, beams = ca.shape
    w_cos = ca[:, None, :, :] * cb[:, :, None, :] - sa[:, None, :, :] * sb[:, :, None, :]
    w_sin = sa[:, None, :, :] * cb[:, :, None, :] + ca[:, None, :, :] * sb[:, :, None, :]
    w_cos = w_cos.reshape(n_chan, GRID * GRID, beams).astype(jnp.bfloat16)
    w_sin = w_sin.reshape(n_chan, GRID * GRID, beams).astype(jnp.bfloat16)
    return w_cos, w_sin


def dft_table(bins):
    sample = jnp.arange(bins, dtype=jnp.int32)
    harmonic = jnp.arange(bins // 2, dtype=jnp.int32) + 1
    turn_count = sample[:, None] * harmonic[None, :] % bins
    angles = turn_count.astype(jnp.float32) * (2.0 * math.pi / bins)
    norm_scale = 1.0 / math.sqrt(bins)
    both = jnp.stack([jnp.cos(angles) * norm_scale, -jnp.sin(angles) * norm_scale], axis=2)
    return both.reshape(bins, bins)


def channel_lags(chan_map, channel_count):
    freq_index = 2 * channel_count - chan_map
    top_square = 2 * channel_count * (2 * channel_count) * 64
    return top_square // (freq_index * freq_index) - 64


def dedisp_kernel(resid_ref, tab_ref, spec_ref, out_ref, lhs_buf, rhs_buf, *, channels):
    rows = resid_ref.shape[0]
    cos_t = jnp.broadcast_to(tab_ref[0, 0:1, :], (rows, 128))
    sin_t = jnp.broadcast_to(tab_ref[0, 1:2, :], (rows, 128))
    for c in range(channels // 128):
        idx = resid_ref[:, c * 128:(c + 1) * 128]
        lhs_buf[:, c * 128:(c + 1) * 128] = jnp.take_along_axis(cos_t, idx, axis=1).astype(jnp.bfloat16)
        lhs_buf[:, channels + c * 128:channels + (c + 1) * 128] = (
            jnp.take_along_axis(sin_t, idx, axis=1).astype(jnp.bfloat16)
        )
    beams = spec_ref.shape[3]
    s_re = spec_ref[0, 0]
    s_im = spec_ref[0, 1]
    rhs_buf[0:channels, 0:beams] = s_re
    rhs_buf[0:channels, beams:2 * beams] = s_im
    rhs_buf[channels:2 * channels, 0:beams] = -s_im
    rhs_buf[channels:2 * channels, beams:2 * beams] = s_re
    res = jnp.dot(lhs_buf[...], rhs_buf[...], preferred_element_type=jnp.float32)
    ded_re = res[:, 0:beams]
    ded_im = res[:, beams:2 * beams]
    out_ref[0] = (ded_re * ded_re + ded_im * ded_im) / channels


def dedisperse(kp1, dm_list, lags, spec, bins):
    n_freq, _, channels, beams = spec.shape
    trials = dm_list.shape[0]
    resid = ((dm_list[:, None] * lags[None, :]) // 4096) % bins
    sample = jnp.arange(128, dtype=jnp.int32) % bins
    turns = (kp1[:, None] * sample[None, :]) % bins
    angles = turns.astype(jnp.float32) * (2.0 * math.pi / bins)
    tab = jnp.zeros((n_freq, 8, 128), jnp.float32)
    tab = tab.at[:, 0].set(jnp.cos(angles).astype(jnp.bfloat16).astype(jnp.float32))
    tab = tab.at[:, 1].set(jnp.sin(angles).astype(jnp.bfloat16).astype(jnp.float32))
    flops = 8 * n_freq * trials * channels * beams
    cost = pl.CostEstimate(
        flops=flops,
        transcendentals=0,
        bytes_accessed=trials * channels * 4 + n_freq * 2 * channels * beams * 2 + n_freq * trials * beams * 4,
    )
    return pl.pallas_call(
        partial(dedisp_kernel, channels=channels),
        out_shape=jax.ShapeDtypeStruct((n_freq, trials, beams), jnp.float32),
        grid=(n_freq,),
        in_specs=[
            pl.BlockSpec((trials, channels), lambda i: (0, 0)),
            pl.BlockSpec((1, 8, 128), lambda i: (i, 0, 0)),
            pl.BlockSpec((1, 2, channels, beams), lambda i: (i, 0, 0, 0)),
        ],
        out_specs=pl.BlockSpec((1, trials, beams), lambda i: (i, 0, 0)),
        scratch_shapes=[
            pltpu.VMEM((trials, 2 * channels), jnp.bfloat16),
            pltpu.VMEM((2 * channels, 2 * beams), jnp.bfloat16),
        ],
        compiler_params=pltpu.CompilerParams(vmem_limit_bytes=48 * 1024 * 1024),
        cost_estimate=cost,
    )(resid, tab, spec)


def beamform(volt_block, nu, beam_pos):
    n_chan, _, samples, antennas = volt_block.shape
    beams = beam_pos.shape[0]
    cos_w, sin_w = steering(nu, beam_pos, antennas)
    cosine_term = jnp.einsum("cpsa,cab->cpsb", volt_block, cos_w, preferred_element_type=jnp.float32)
    sin_part = jnp.einsum("cpsa,cab->cpsb", volt_block, sin_w, preferred_element_type=jnp.float32)
    real_part = cosine_term[:, 0] + sin_part[:, 1]
    imag_part = cosine_term[:, 1] - sin_part[:, 0]
    power_now = real_part * real_part + imag_part * imag_part
    return jnp.mean(power_now.reshape(n_chan, samples // 4, 4, beams), axis=2)


def spectra_of(history, fresh_bins):
    highest = lax.Precision.HIGHEST
    window = jnp.concatenate([history, fresh_bins], axis=1)
    bins = window.shape[1]
    scaled = window / (jnp.mean(window, axis=1, keepdims=True) + 1e-06)
    spectra = jnp.einsum("ctb,tj->jcb", scaled, dft_table(bins), precision=highest).astype(jnp.bfloat16)
    return spectra.reshape(bins // 2, 2, history.shape[0], history.shape[2])


def local(voltages, history, beam_pos, dm_list, chan_map):
    devices = lax.axis_size("gx")
    channel_count = devices * chan_map.shape[0]
    local_chan = voltages.shape[0]
    block_size = math.gcd(local_chan, 8)
    n_blocks = local_chan // block_size
    volt_blocks = voltages.reshape(n_blocks, block_size, *voltages.shape[1:])
    freq_blocks = (2 * channel_count - chan_map).reshape(n_blocks, block_size)
    all_chan = lax.all_gather(chan_map, "gx", axis=0, tiled=True)
    all_chan, volt_blocks = lax.optimization_barrier((all_chan, volt_blocks))
    fresh = [beamform(volt_blocks[i], freq_blocks[i], beam_pos) for i in range(n_blocks)]
    fresh_bins = jnp.concatenate(fresh, axis=0)
    spectra = spectra_of(history, fresh_bins)
    bins = 2 * spectra.shape[0]
    turned = lax.all_to_all(spectra, "gx", split_axis=0, concat_axis=2, tiled=True)
    freq_dev = turned.shape[0]
    lags = channel_lags(all_chan, channel_count)
    kp1 = lax.axis_index("gx") * freq_dev + jnp.arange(freq_dev, dtype=jnp.int32) + 1
    return dedisperse(kp1, dm_list, lags, turned, bins)


def solution(mesh):
    in_specs = (
        P(("groups", "gx"), None, None, None),
        P(("groups", "gx"), None, None),
        P(),
        P(),
        P("gx"),
    )
    out_specs = P(("groups", "gx"), None, None)
    return jax.shard_map(local, mesh=mesh, in_specs=in_specs, out_specs=out_specs, check_vma=False)
```

```python
from functools import partial
import math

import jax
import jax.numpy as jnp
from jax import lax
from jax.experimental import pallas as pl
from jax.experimental.pallas import tpu as pltpu
from jax.sharding import PartitionSpec as P

GRID = 32
PHASES = 8192


def axis_tables(nu, pos, scale):
    step = (nu[:, None] * pos[None, :]) % PHASES

    def trig(mult, factor):
        turns = (step[:, None, :] * (mult[None, :, None] * factor)) % PHASES
        angles = turns.astype(jnp.float32) * (2.0 * math.pi / PHASES)
        return jnp.cos(angles), jnp.sin(angles)

    lo = jnp.arange(8, dtype=jnp.int32)
    hi = jnp.arange(GRID // 8, dtype=jnp.int32)
    c_lo, s_lo = trig(lo, 1)
    c_hi, s_hi = trig(hi, 8)
    cos_t = c_hi[:, :, None, :] * c_lo[:, None, :, :] - s_hi[:, :, None, :] * s_lo[:, None, :, :]
    sin_t = s_hi[:, :, None, :] * c_lo[:, None, :, :] + c_hi[:, :, None, :] * s_lo[:, None, :, :]
    shape = (nu.shape[0], GRID, pos.shape[0])
    return cos_t.reshape(shape) * scale, sin_t.reshape(shape) * scale


def steering(nu, beam_pos, antennas):
    weight_scale = 1.0 / math.sqrt(antennas)
    ca, sa = axis_tables(nu, beam_pos[:, 0], weight_scale)
    cb, sb = axis_tables(nu, beam_pos[:, 1], 1.0)
    n_chan, _, beams = ca.shape
    w_cos = ca[:, None, :, :] * cb[:, :, None, :] - sa[:, None, :, :] * sb[:, :, None, :]
    w_sin = sa[:, None, :, :] * cb[:, :, None, :] + ca[:, None, :, :] * sb[:, :, None, :]
    w_cos = w_cos.reshape(n_chan, GRID * GRID, beams).astype(jnp.bfloat16)
    w_sin = w_sin.reshape(n_chan, GRID * GRID, beams).astype(jnp.bfloat16)
    return w_cos, w_sin


def dft_table(bins):
    sample = jnp.arange(bins, dtype=jnp.int32)
    harmonic = jnp.arange(bins // 2, dtype=jnp.int32) + 1
    turn_count = sample[:, None] * harmonic[None, :] % bins
    angles = turn_count.astype(jnp.float32) * (2.0 * math.pi / bins)
    norm_scale = 1.0 / math.sqrt(bins)
    both = jnp.stack([jnp.cos(angles) * norm_scale, -jnp.sin(angles) * norm_scale], axis=2)
    return both.reshape(bins, bins)


def channel_lags(chan_map, channel_count):
    freq_index = 2 * channel_count - chan_map
    top_square = 2 * channel_count * (2 * channel_count) * 64
    return top_square // (freq_index * freq_index) - 64


def dedisp_kernel(resid_ref, tab_ref, spec_ref, out_ref, lhs_buf, rhs_buf, *, channels):
    rows = resid_ref.shape[0]
    cos_t = jnp.broadcast_to(tab_ref[0, 0:1, :], (rows, 128))
    sin_t = jnp.broadcast_to(tab_ref[0, 1:2, :], (rows, 128))
    for c in range(channels // 128):
        idx = resid_ref[:, c * 128:(c + 1) * 128]
        lhs_buf[:, c * 128:(c + 1) * 128] = jnp.take_along_axis(cos_t, idx, axis=1).astype(jnp.bfloat16)
        lhs_buf[:, channels + c * 128:channels + (c + 1) * 128] = (
            jnp.take_along_axis(sin_t, idx, axis=1).astype(jnp.bfloat16)
        )
    beams = spec_ref.shape[3]
    s_re = spec_ref[0, 0]
    s_im = spec_ref[0, 1]
    rhs_buf[0:channels, 0:beams] = s_re
    rhs_buf[0:channels, beams:2 * beams] = s_im
    rhs_buf[channels:2 * channels, 0:beams] = -s_im
    rhs_buf[channels:2 * channels, beams:2 * beams] = s_re
    res = jnp.dot(lhs_buf[...], rhs_buf[...], preferred_element_type=jnp.float32)
    ded_re = res[:, 0:beams]
    ded_im = res[:, beams:2 * beams]
    out_ref[0] = (ded_re * ded_re + ded_im * ded_im) / channels


def dedisperse(kp1, dm_list, lags, spec, bins):
    n_freq, _, channels, beams = spec.shape
    trials = dm_list.shape[0]
    resid = ((dm_list[:, None] * lags[None, :]) // 4096) % bins
    sample = jnp.arange(128, dtype=jnp.int32) % bins
    turns = (kp1[:, None] * sample[None, :]) % bins
    angles = turns.astype(jnp.float32) * (2.0 * math.pi / bins)
    tab = jnp.zeros((n_freq, 8, 128), jnp.float32)
    tab = tab.at[:, 0].set(jnp.cos(angles).astype(jnp.bfloat16).astype(jnp.float32))
    tab = tab.at[:, 1].set(jnp.sin(angles).astype(jnp.bfloat16).astype(jnp.float32))
    flops = 8 * n_freq * trials * channels * beams
    cost = pl.CostEstimate(
        flops=flops,
        transcendentals=0,
        bytes_accessed=trials * channels * 4 + n_freq * 2 * channels * beams * 2 + n_freq * trials * beams * 4,
    )
    return pl.pallas_call(
        partial(dedisp_kernel, channels=channels),
        out_shape=jax.ShapeDtypeStruct((n_freq, trials, beams), jnp.float32),
        grid=(n_freq,),
        in_specs=[
            pl.BlockSpec((trials, channels), lambda i: (0, 0)),
            pl.BlockSpec((1, 8, 128), lambda i: (i, 0, 0)),
            pl.BlockSpec((1, 2, channels, beams), lambda i: (i, 0, 0, 0)),
        ],
        out_specs=pl.BlockSpec((1, trials, beams), lambda i: (i, 0, 0)),
        scratch_shapes=[
            pltpu.VMEM((trials, 2 * channels), jnp.bfloat16),
            pltpu.VMEM((2 * channels, 2 * beams), jnp.bfloat16),
        ],
        compiler_params=pltpu.CompilerParams(vmem_limit_bytes=48 * 1024 * 1024),
        cost_estimate=cost,
    )(resid, tab, spec)


def beamform(volt_block, nu, beam_pos):
    n_chan, _, samples, antennas = volt_block.shape
    beams = beam_pos.shape[0]
    cos_w, sin_w = steering(nu, beam_pos, antennas)
    cosine_term = jnp.einsum("cpsa,cab->cpsb", volt_block, cos_w, preferred_element_type=jnp.float32)
    sin_part = jnp.einsum("cpsa,cab->cpsb", volt_block, sin_w, preferred_element_type=jnp.float32)
    real_part = cosine_term[:, 0] + sin_part[:, 1]
    imag_part = cosine_term[:, 1] - sin_part[:, 0]
    power_now = real_part * real_part + imag_part * imag_part
    return jnp.mean(power_now.reshape(n_chan, samples // 4, 4, beams), axis=2)


def spectra_of(history, fresh_bins):
    highest = lax.Precision.HIGHEST
    window = jnp.concatenate([history, fresh_bins], axis=1)
    bins = window.shape[1]
    scaled = window / (jnp.mean(window, axis=1, keepdims=True) + 1e-06)
    spectra = jnp.einsum("ctb,tj->jcb", scaled, dft_table(bins), precision=highest).astype(jnp.bfloat16)
    return spectra.reshape(bins // 2, 2, history.shape[0], history.shape[2])


def local(voltages, history, beam_pos, dm_list, chan_map):
    devices = lax.axis_size("gx")
    channel_count = devices * chan_map.shape[0]
    local_chan = voltages.shape[0]
    block_size = math.gcd(local_chan, 8)
    n_blocks = local_chan // block_size
    volt_blocks = voltages.reshape(n_blocks, block_size, *voltages.shape[1:])
    freq_blocks = (2 * channel_count - chan_map).reshape(n_blocks, block_size)
    fresh = [beamform(volt_blocks[i], freq_blocks[i], beam_pos) for i in range(n_blocks)]
    fresh_bins = jnp.concatenate(fresh, axis=0)
    spectra = spectra_of(history, fresh_bins)
    freqs, _, _, beams = spectra.shape
    bins = 2 * freqs
    freq_dev = freqs // devices
    own_lags = channel_lags(chan_map, channel_count).astype(jnp.bfloat16)
    body = spectra.reshape(devices, freq_dev * 2 * local_chan * beams)
    tail = jnp.zeros((devices, 128), jnp.bfloat16).at[:, :local_chan].set(own_lags[None, :])
    payload = jnp.concatenate([body, tail], axis=1)
    got = lax.all_to_all(payload, "gx", split_axis=0, concat_axis=0, tiled=True)
    turned = got[:, : body.shape[1]].reshape(devices, freq_dev, 2, local_chan, beams)
    turned = turned.transpose(1, 2, 0, 3, 4).reshape(freq_dev, 2, channel_count, beams)
    lags = got[:, body.shape[1]:body.shape[1] + local_chan].astype(jnp.int32).reshape(channel_count)
    kp1 = lax.axis_index("gx") * freq_dev + jnp.arange(freq_dev, dtype=jnp.int32) + 1
    return dedisperse(kp1, dm_list, lags, turned, bins)


def solution(mesh):
    in_specs = (
        P(("groups", "gx"), None, None, None),
        P(("groups", "gx"), None, None),
        P(),
        P(),
        P("gx"),
    )
    out_specs = P(("groups", "gx"), None, None)
    return jax.shard_map(local, mesh=mesh, in_specs=in_specs, out_specs=out_specs, check_vma=False)
```

```python
from functools import partial
import math

import jax
import jax.numpy as jnp
from jax import lax
from jax.experimental import pallas as pl
from jax.experimental.pallas import tpu as pltpu
from jax.sharding import PartitionSpec as P

GRID = 32
PHASES = 8192


def axis_tables(nu, pos, scale):
    step = (nu[:, None] * pos[None, :]) % PHASES

    def trig(mult, factor):
        turns = (step[:, None, :] * (mult[None, :, None] * factor)) % PHASES
        angles = turns.astype(jnp.float32) * (2.0 * math.pi / PHASES)
        return jnp.cos(angles), jnp.sin(angles)

    lo = jnp.arange(8, dtype=jnp.int32)
    hi = jnp.arange(GRID // 8, dtype=jnp.int32)
    c_lo, s_lo = trig(lo, 1)
    c_hi, s_hi = trig(hi, 8)
    cos_t = c_hi[:, :, None, :] * c_lo[:, None, :, :] - s_hi[:, :, None, :] * s_lo[:, None, :, :]
    sin_t = s_hi[:, :, None, :] * c_lo[:, None, :, :] + c_hi[:, :, None, :] * s_lo[:, None, :, :]
    shape = (nu.shape[0], GRID, pos.shape[0])
    return cos_t.reshape(shape) * scale, sin_t.reshape(shape) * scale


def steering(nu, beam_pos, antennas):
    weight_scale = 1.0 / math.sqrt(antennas)
    ca, sa = axis_tables(nu, beam_pos[:, 0], weight_scale)
    cb, sb = axis_tables(nu, beam_pos[:, 1], 1.0)
    n_chan, _, beams = ca.shape
    w_cos = ca[:, None, :, :] * cb[:, :, None, :] - sa[:, None, :, :] * sb[:, :, None, :]
    w_sin = sa[:, None, :, :] * cb[:, :, None, :] + ca[:, None, :, :] * sb[:, :, None, :]
    w_cos = w_cos.reshape(n_chan, GRID * GRID, beams).astype(jnp.bfloat16)
    w_sin = w_sin.reshape(n_chan, GRID * GRID, beams).astype(jnp.bfloat16)
    return w_cos, w_sin


def dft_table(bins):
    sample = jnp.arange(bins, dtype=jnp.int32)
    harmonic = jnp.arange(bins // 2, dtype=jnp.int32) + 1
    turn_count = sample[:, None] * harmonic[None, :] % bins
    angles = turn_count.astype(jnp.float32) * (2.0 * math.pi / bins)
    norm_scale = 1.0 / math.sqrt(bins)
    both = jnp.stack([jnp.cos(angles) * norm_scale, -jnp.sin(angles) * norm_scale], axis=2)
    return both.reshape(bins, bins)


def channel_lags(chan_map, channel_count):
    freq_index = 2 * channel_count - chan_map
    top_square = 2 * channel_count * (2 * channel_count) * 64
    return top_square // (freq_index * freq_index) - 64


def dedisp_kernel(resid_ref, tab_ref, spec_ref, out_ref, lhs_buf, rhs_buf, *, channels):
    rows = resid_ref.shape[0]
    cos_t = jnp.broadcast_to(tab_ref[0, 0:1, :], (rows, 128))
    sin_t = jnp.broadcast_to(tab_ref[0, 1:2, :], (rows, 128))
    for c in range(channels // 128):
        idx = resid_ref[:, c * 128:(c + 1) * 128]
        lhs_buf[:, c * 128:(c + 1) * 128] = jnp.take_along_axis(cos_t, idx, axis=1).astype(jnp.bfloat16)
        lhs_buf[:, channels + c * 128:channels + (c + 1) * 128] = (
            jnp.take_along_axis(sin_t, idx, axis=1).astype(jnp.bfloat16)
        )
    beams = spec_ref.shape[3]
    s_re = spec_ref[0, 0]
    s_im = spec_ref[0, 1]
    rhs_buf[0:channels, 0:beams] = s_re
    rhs_buf[0:channels, beams:2 * beams] = s_im
    rhs_buf[channels:2 * channels, 0:beams] = -s_im
    rhs_buf[channels:2 * channels, beams:2 * beams] = s_re
    res = jnp.dot(lhs_buf[...], rhs_buf[...], preferred_element_type=jnp.float32)
    ded_re = res[:, 0:beams]
    ded_im = res[:, beams:2 * beams]
    out_ref[0] = (ded_re * ded_re + ded_im * ded_im) / channels


def dedisperse(kp1, dm_list, lags, spec, bins):
    n_freq, _, channels, beams = spec.shape
    trials = dm_list.shape[0]
    resid = ((dm_list[:, None] * lags[None, :]) // 4096) % bins
    sample = jnp.arange(128, dtype=jnp.int32) % bins
    turns = (kp1[:, None] * sample[None, :]) % bins
    angles = turns.astype(jnp.float32) * (2.0 * math.pi / bins)
    tab = jnp.zeros((n_freq, 8, 128), jnp.float32)
    tab = tab.at[:, 0].set(jnp.cos(angles).astype(jnp.bfloat16).astype(jnp.float32))
    tab = tab.at[:, 1].set(jnp.sin(angles).astype(jnp.bfloat16).astype(jnp.float32))
    flops = 8 * n_freq * trials * channels * beams
    cost = pl.CostEstimate(
        flops=flops,
        transcendentals=0,
        bytes_accessed=trials * channels * 4 + n_freq * 2 * channels * beams * 2 + n_freq * trials * beams * 4,
    )
    return pl.pallas_call(
        partial(dedisp_kernel, channels=channels),
        out_shape=jax.ShapeDtypeStruct((n_freq, trials, beams), jnp.float32),
        grid=(n_freq,),
        in_specs=[
            pl.BlockSpec((trials, channels), lambda i: (0, 0)),
            pl.BlockSpec((1, 8, 128), lambda i: (i, 0, 0)),
            pl.BlockSpec((1, 2, channels, beams), lambda i: (i, 0, 0, 0)),
        ],
        out_specs=pl.BlockSpec((1, trials, beams), lambda i: (i, 0, 0)),
        scratch_shapes=[
            pltpu.VMEM((trials, 2 * channels), jnp.bfloat16),
            pltpu.VMEM((2 * channels, 2 * beams), jnp.bfloat16),
        ],
        compiler_params=pltpu.CompilerParams(vmem_limit_bytes=48 * 1024 * 1024),
        cost_estimate=cost,
    )(resid, tab, spec)


def beamform(volt_block, nu, beam_pos):
    n_chan, _, samples, antennas = volt_block.shape
    beams = beam_pos.shape[0]
    cos_w, sin_w = steering(nu, beam_pos, antennas)
    cosine_term = jnp.einsum("cpsa,cab->cpsb", volt_block, cos_w, preferred_element_type=jnp.float32)
    sin_part = jnp.einsum("cpsa,cab->cpsb", volt_block, sin_w, preferred_element_type=jnp.float32)
    real_part = cosine_term[:, 0] + sin_part[:, 1]
    imag_part = cosine_term[:, 1] - sin_part[:, 0]
    power_now = real_part * real_part + imag_part * imag_part
    return jnp.mean(power_now.reshape(n_chan, samples // 4, 4, beams), axis=2)


def spectra_of(history, fresh_bins):
    highest = lax.Precision.HIGHEST
    window = jnp.concatenate([history, fresh_bins], axis=1)
    bins = window.shape[1]
    scale = jnp.mean(window, axis=1) + 1e-06
    raw = jnp.einsum("ctb,tj->jcb", window, dft_table(bins), precision=highest)
    spectra = (raw / scale[None]).astype(jnp.bfloat16)
    return spectra.reshape(bins // 2, 2, history.shape[0], history.shape[2])


def local(voltages, history, beam_pos, dm_list, chan_map):
    devices = lax.axis_size("gx")
    channel_count = devices * chan_map.shape[0]
    local_chan = voltages.shape[0]
    block_size = math.gcd(local_chan, 8)
    n_blocks = local_chan // block_size
    volt_blocks = voltages.reshape(n_blocks, block_size, *voltages.shape[1:])
    freq_blocks = (2 * channel_count - chan_map).reshape(n_blocks, block_size)
    all_chan = lax.all_gather(chan_map, "gx", axis=0, tiled=True)
    all_chan, volt_blocks = lax.optimization_barrier((all_chan, volt_blocks))
    fresh = [beamform(volt_blocks[i], freq_blocks[i], beam_pos) for i in range(n_blocks)]
    fresh_bins = jnp.concatenate(fresh, axis=0)
    spectra = spectra_of(history, fresh_bins)
    bins = 2 * spectra.shape[0]
    turned = lax.all_to_all(spectra, "gx", split_axis=0, concat_axis=2, tiled=True)
    freq_dev = turned.shape[0]
    lags = channel_lags(all_chan, channel_count)
    kp1 = lax.axis_index("gx") * freq_dev + jnp.arange(freq_dev, dtype=jnp.int32) + 1
    return dedisperse(kp1, dm_list, lags, turned, bins)


def solution(mesh):
    in_specs = (
        P(("groups", "gx"), None, None, None),
        P(("groups", "gx"), None, None),
        P(),
        P(),
        P("gx"),
    )
    out_specs = P(("groups", "gx"), None, None)
    return jax.shard_map(local, mesh=mesh, in_specs=in_specs, out_specs=out_specs, check_vma=False)
```

```python
from functools import partial
import math

import jax
import jax.numpy as jnp
from jax import lax
from jax.experimental import pallas as pl
from jax.experimental.pallas import tpu as pltpu
from jax.sharding import PartitionSpec as P

GRID = 32
PHASES = 8192


def axis_tables(nu, pos, scale):
    step = (nu[:, None] * pos[None, :]) % PHASES

    def trig(mult, factor):
        turns = (step[:, None, :] * (mult[None, :, None] * factor)) % PHASES
        angles = turns.astype(jnp.float32) * (2.0 * math.pi / PHASES)
        return jnp.cos(angles), jnp.sin(angles)

    lo = jnp.arange(8, dtype=jnp.int32)
    hi = jnp.arange(GRID // 8, dtype=jnp.int32)
    c_lo, s_lo = trig(lo, 1)
    c_hi, s_hi = trig(hi, 8)
    cos_t = c_hi[:, :, None, :] * c_lo[:, None, :, :] - s_hi[:, :, None, :] * s_lo[:, None, :, :]
    sin_t = s_hi[:, :, None, :] * c_lo[:, None, :, :] + c_hi[:, :, None, :] * s_lo[:, None, :, :]
    shape = (nu.shape[0], GRID, pos.shape[0])
    return cos_t.reshape(shape) * scale, sin_t.reshape(shape) * scale


def steering(nu, beam_pos, antennas):
    weight_scale = 1.0 / math.sqrt(antennas)
    ca, sa = axis_tables(nu, beam_pos[:, 0], weight_scale)
    cb, sb = axis_tables(nu, beam_pos[:, 1], 1.0)
    n_chan, _, beams = ca.shape
    w_cos = ca[:, None, :, :] * cb[:, :, None, :] - sa[:, None, :, :] * sb[:, :, None, :]
    w_sin = sa[:, None, :, :] * cb[:, :, None, :] + ca[:, None, :, :] * sb[:, :, None, :]
    w_cos = w_cos.reshape(n_chan, GRID * GRID, beams).astype(jnp.bfloat16)
    w_sin = w_sin.reshape(n_chan, GRID * GRID, beams).astype(jnp.bfloat16)
    return w_cos, w_sin


def dft_table(bins):
    sample = jnp.arange(bins, dtype=jnp.int32)
    harmonic = jnp.arange(bins // 2, dtype=jnp.int32) + 1
    turn_count = sample[:, None] * harmonic[None, :] % bins
    angles = turn_count.astype(jnp.float32) * (2.0 * math.pi / bins)
    norm_scale = 1.0 / math.sqrt(bins)
    both = jnp.stack([jnp.cos(angles) * norm_scale, -jnp.sin(angles) * norm_scale], axis=2)
    return both.reshape(bins, bins)


def channel_lags(chan_map, channel_count):
    freq_index = 2 * channel_count - chan_map
    top_square = 2 * channel_count * (2 * channel_count) * 64
    return top_square // (freq_index * freq_index) - 64


def dedisp_kernel(resid_ref, tab_ref, spec_ref, out_ref, lhs_buf, rhs_buf, *, channels):
    rows = resid_ref.shape[0]
    cos_t = jnp.broadcast_to(tab_ref[0, 0:1, :], (rows, 128))
    sin_t = jnp.broadcast_to(tab_ref[0, 1:2, :], (rows, 128))
    for c in range(channels // 128):
        idx = resid_ref[:, c * 128:(c + 1) * 128]
        lhs_buf[:, c * 128:(c + 1) * 128] = jnp.take_along_axis(cos_t, idx, axis=1).astype(jnp.bfloat16)
        lhs_buf[:, channels + c * 128:channels + (c + 1) * 128] = (
            jnp.take_along_axis(sin_t, idx, axis=1).astype(jnp.bfloat16)
        )
    beams = spec_ref.shape[3]
    s_re = spec_ref[0, 0]
    s_im = spec_ref[0, 1]
    rhs_buf[0:channels, 0:beams] = s_re
    rhs_buf[0:channels, beams:2 * beams] = s_im
    rhs_buf[channels:2 * channels, 0:beams] = -s_im
    rhs_buf[channels:2 * channels, beams:2 * beams] = s_re
    res = jnp.dot(lhs_buf[...], rhs_buf[...], preferred_element_type=jnp.float32)
    ded_re = res[:, 0:beams]
    ded_im = res[:, beams:2 * beams]
    out_ref[0] = (ded_re * ded_re + ded_im * ded_im) / channels


def dedisperse(kp1, dm_list, lags, spec, bins):
    n_freq, _, channels, beams = spec.shape
    trials = dm_list.shape[0]
    resid = ((dm_list[:, None] * lags[None, :]) // 4096) % bins
    sample = jnp.arange(128, dtype=jnp.int32) % bins
    turns = (kp1[:, None] * sample[None, :]) % bins
    angles = turns.astype(jnp.float32) * (2.0 * math.pi / bins)
    tab = jnp.zeros((n_freq, 8, 128), jnp.float32)
    tab = tab.at[:, 0].set(jnp.cos(angles).astype(jnp.bfloat16).astype(jnp.float32))
    tab = tab.at[:, 1].set(jnp.sin(angles).astype(jnp.bfloat16).astype(jnp.float32))
    flops = 8 * n_freq * trials * channels * beams
    cost = pl.CostEstimate(
        flops=flops,
        transcendentals=0,
        bytes_accessed=trials * channels * 4 + n_freq * 2 * channels * beams * 2 + n_freq * trials * beams * 4,
    )
    return pl.pallas_call(
        partial(dedisp_kernel, channels=channels),
        out_shape=jax.ShapeDtypeStruct((n_freq, trials, beams), jnp.float32),
        grid=(n_freq,),
        in_specs=[
            pl.BlockSpec((trials, channels), lambda i: (0, 0)),
            pl.BlockSpec((1, 8, 128), lambda i: (i, 0, 0)),
            pl.BlockSpec((1, 2, channels, beams), lambda i: (i, 0, 0, 0)),
        ],
        out_specs=pl.BlockSpec((1, trials, beams), lambda i: (i, 0, 0)),
        scratch_shapes=[
            pltpu.VMEM((trials, 2 * channels), jnp.bfloat16),
            pltpu.VMEM((2 * channels, 2 * beams), jnp.bfloat16),
        ],
        compiler_params=pltpu.CompilerParams(vmem_limit_bytes=48 * 1024 * 1024),
        cost_estimate=cost,
    )(resid, tab, spec)


def beamform(volt_block, nu, beam_pos):
    n_chan, _, samples, antennas = volt_block.shape
    beams = beam_pos.shape[0]
    cos_w, sin_w = steering(nu, beam_pos, antennas)
    cosine_term = jnp.einsum("cpsa,cab->cpsb", volt_block, cos_w, preferred_element_type=jnp.float32)
    sin_part = jnp.einsum("cpsa,cab->cpsb", volt_block, sin_w, preferred_element_type=jnp.float32)
    real_part = cosine_term[:, 0] + sin_part[:, 1]
    imag_part = cosine_term[:, 1] - sin_part[:, 0]
    power_now = real_part * real_part + imag_part * imag_part
    return jnp.mean(power_now.reshape(n_chan, samples // 4, 4, beams), axis=2)


def spectra_of(history, fresh_bins):
    highest = lax.Precision.HIGHEST
    window = jnp.concatenate([history, fresh_bins], axis=1)
    bins = window.shape[1]
    scaled = window / (jnp.mean(window, axis=1, keepdims=True) + 1e-06)
    spectra = jnp.einsum("ctb,tj->jcb", scaled, dft_table(bins), precision=highest).astype(jnp.bfloat16)
    return spectra.reshape(bins // 2, 2, history.shape[0], history.shape[2])


def local(voltages, history, beam_pos, dm_list, chan_map):
    devices = lax.axis_size("gx")
    channel_count = devices * chan_map.shape[0]
    local_chan = voltages.shape[0]
    block_size = math.gcd(local_chan, 8)
    n_blocks = local_chan // block_size
    volt_blocks = voltages.reshape(n_blocks, block_size, *voltages.shape[1:])
    freq_blocks = (2 * channel_count - chan_map).reshape(n_blocks, block_size)
    tile = jnp.zeros((1, 8, 128), jnp.float32).at[0, 0, : chan_map.shape[0]].set(chan_map.astype(jnp.float32))
    gathered = lax.all_gather(tile, "gx", axis=0, tiled=True)
    all_chan = gathered[:, 0, : chan_map.shape[0]].reshape(-1).astype(jnp.int32)
    all_chan, volt_blocks = lax.optimization_barrier((all_chan, volt_blocks))
    fresh = [beamform(volt_blocks[i], freq_blocks[i], beam_pos) for i in range(n_blocks)]
    fresh_bins = jnp.concatenate(fresh, axis=0)
    spectra = spectra_of(history, fresh_bins)
    bins = 2 * spectra.shape[0]
    turned = lax.all_to_all(spectra, "gx", split_axis=0, concat_axis=2, tiled=True)
    freq_dev = turned.shape[0]
    lags = channel_lags(all_chan, channel_count)
    kp1 = lax.axis_index("gx") * freq_dev + jnp.arange(freq_dev, dtype=jnp.int32) + 1
    return dedisperse(kp1, dm_list, lags, turned, bins)


def solution(mesh):
    in_specs = (
        P(("groups", "gx"), None, None, None),
        P(("groups", "gx"), None, None),
        P(),
        P(),
        P("gx"),
    )
    out_specs = P(("groups", "gx"), None, None)
    return jax.shard_map(local, mesh=mesh, in_specs=in_specs, out_specs=out_specs, check_vma=False)
```

```python
from functools import partial
import math

import jax
import jax.numpy as jnp
from jax import lax
from jax.experimental import pallas as pl
from jax.experimental.pallas import tpu as pltpu
from jax.sharding import PartitionSpec as P

GRID = 32
PHASES = 8192


def axis_tables(nu, pos, scale):
    step = (nu[:, None] * pos[None, :]) % PHASES

    def trig(mult, factor):
        turns = (step[:, None, :] * (mult[None, :, None] * factor)) % PHASES
        angles = turns.astype(jnp.float32) * (2.0 * math.pi / PHASES)
        return jnp.cos(angles), jnp.sin(angles)

    lo = jnp.arange(8, dtype=jnp.int32)
    hi = jnp.arange(GRID // 8, dtype=jnp.int32)
    c_lo, s_lo = trig(lo, 1)
    c_hi, s_hi = trig(hi, 8)
    cos_t = c_hi[:, :, None, :] * c_lo[:, None, :, :] - s_hi[:, :, None, :] * s_lo[:, None, :, :]
    sin_t = s_hi[:, :, None, :] * c_lo[:, None, :, :] + c_hi[:, :, None, :] * s_lo[:, None, :, :]
    shape = (nu.shape[0], GRID, pos.shape[0])
    return cos_t.reshape(shape) * scale, sin_t.reshape(shape) * scale


def steering(nu, beam_pos, antennas):
    weight_scale = 1.0 / math.sqrt(antennas)
    ca, sa = axis_tables(nu, beam_pos[:, 0], weight_scale)
    cb, sb = axis_tables(nu, beam_pos[:, 1], 1.0)
    n_chan, _, beams = ca.shape
    w_cos = ca[:, None, :, :] * cb[:, :, None, :] - sa[:, None, :, :] * sb[:, :, None, :]
    w_sin = sa[:, None, :, :] * cb[:, :, None, :] + ca[:, None, :, :] * sb[:, :, None, :]
    w_cos = w_cos.reshape(n_chan, GRID * GRID, beams).astype(jnp.bfloat16)
    w_sin = w_sin.reshape(n_chan, GRID * GRID, beams).astype(jnp.bfloat16)
    return w_cos, w_sin


def dft_table(bins):
    sample = jnp.arange(bins, dtype=jnp.int32)
    harmonic = jnp.arange(bins // 2, dtype=jnp.int32) + 1
    turn_count = sample[:, None] * harmonic[None, :] % bins
    angles = turn_count.astype(jnp.float32) * (2.0 * math.pi / bins)
    norm_scale = 1.0 / math.sqrt(bins)
    both = jnp.stack([jnp.cos(angles) * norm_scale, -jnp.sin(angles) * norm_scale], axis=2)
    return both.reshape(bins, bins)


def channel_lags(chan_map, channel_count):
    freq_index = 2 * channel_count - chan_map
    top_square = 2 * channel_count * (2 * channel_count) * 64
    return top_square // (freq_index * freq_index) - 64


def dedisp_kernel(resid_ref, tab_ref, spec_ref, out_ref, lhs_buf, rhs_buf, *, channels):
    rows = resid_ref.shape[0]
    cos_t = jnp.broadcast_to(tab_ref[0, 0:1, :], (rows, 128))
    sin_t = jnp.broadcast_to(tab_ref[0, 1:2, :], (rows, 128))
    for c in range(channels // 128):
        idx = resid_ref[:, c * 128:(c + 1) * 128]
        lhs_buf[:, c * 128:(c + 1) * 128] = jnp.take_along_axis(cos_t, idx, axis=1).astype(jnp.bfloat16)
        lhs_buf[:, channels + c * 128:channels + (c + 1) * 128] = (
            jnp.take_along_axis(sin_t, idx, axis=1).astype(jnp.bfloat16)
        )
    beams = spec_ref.shape[3]
    s_re = spec_ref[0, 0]
    s_im = spec_ref[0, 1]
    rhs_buf[0:channels, 0:beams] = s_re
    rhs_buf[0:channels, beams:2 * beams] = s_im
    rhs_buf[channels:2 * channels, 0:beams] = -s_im
    rhs_buf[channels:2 * channels, beams:2 * beams] = s_re
    res = jnp.dot(lhs_buf[...], rhs_buf[...], preferred_element_type=jnp.float32)
    ded_re = res[:, 0:beams]
    ded_im = res[:, beams:2 * beams]
    out_ref[0] = (ded_re * ded_re + ded_im * ded_im) / channels


def dedisperse(kp1, dm_list, lags, spec, bins):
    n_freq, _, channels, beams = spec.shape
    trials = dm_list.shape[0]
    resid = ((dm_list[:, None] * lags[None, :]) // 4096) % bins
    sample = jnp.arange(128, dtype=jnp.int32) % bins
    turns = (kp1[:, None] * sample[None, :]) % bins
    angles = turns.astype(jnp.float32) * (2.0 * math.pi / bins)
    tab = jnp.zeros((n_freq, 8, 128), jnp.float32)
    tab = tab.at[:, 0].set(jnp.cos(angles).astype(jnp.bfloat16).astype(jnp.float32))
    tab = tab.at[:, 1].set(jnp.sin(angles).astype(jnp.bfloat16).astype(jnp.float32))
    flops = 8 * n_freq * trials * channels * beams
    cost = pl.CostEstimate(
        flops=flops,
        transcendentals=0,
        bytes_accessed=trials * channels * 4 + n_freq * 2 * channels * beams * 2 + n_freq * trials * beams * 4,
    )
    return pl.pallas_call(
        partial(dedisp_kernel, channels=channels),
        out_shape=jax.ShapeDtypeStruct((n_freq, trials, beams), jnp.float32),
        grid=(n_freq,),
        in_specs=[
            pl.BlockSpec((trials, channels), lambda i: (0, 0)),
            pl.BlockSpec((1, 8, 128), lambda i: (i, 0, 0)),
            pl.BlockSpec((1, 2, channels, beams), lambda i: (i, 0, 0, 0)),
        ],
        out_specs=pl.BlockSpec((1, trials, beams), lambda i: (i, 0, 0)),
        scratch_shapes=[
            pltpu.VMEM((trials, 2 * channels), jnp.bfloat16),
            pltpu.VMEM((2 * channels, 2 * beams), jnp.bfloat16),
        ],
        compiler_params=pltpu.CompilerParams(vmem_limit_bytes=48 * 1024 * 1024),
        cost_estimate=cost,
    )(resid, tab, spec)


def beamform(volt_block, nu, beam_pos):
    n_chan, _, samples, antennas = volt_block.shape
    beams = beam_pos.shape[0]
    cos_w, sin_w = steering(nu, beam_pos, antennas)
    cosine_term = jnp.einsum("cpsa,cab->cpsb", volt_block, cos_w, preferred_element_type=jnp.float32)
    sin_part = jnp.einsum("cpsa,cab->cpsb", volt_block, sin_w, preferred_element_type=jnp.float32)
    real_part = cosine_term[:, 0] + sin_part[:, 1]
    imag_part = cosine_term[:, 1] - sin_part[:, 0]
    power_now = real_part * real_part + imag_part * imag_part
    return jnp.mean(power_now.reshape(n_chan, samples // 4, 4, beams), axis=2)


def spectra_of(history, fresh_bins):
    highest = lax.Precision.HIGHEST
    window = jnp.concatenate([history, fresh_bins], axis=1)
    bins = window.shape[1]
    scaled = window / (jnp.mean(window, axis=1, keepdims=True) + 1e-06)
    spectra = jnp.einsum("ctb,tj->jcb", scaled, dft_table(bins), precision=highest).astype(jnp.bfloat16)
    return spectra.reshape(bins // 2, 2, history.shape[0], history.shape[2])


def local(voltages, history, beam_pos, dm_list, chan_map):
    devices = lax.axis_size("gx")
    channel_count = devices * chan_map.shape[0]
    local_chan = voltages.shape[0]
    block_size = math.gcd(local_chan, 8)
    n_blocks = local_chan // block_size
    volt_blocks = voltages.reshape(n_blocks, block_size, *voltages.shape[1:])
    freq_blocks = (2 * channel_count - chan_map).reshape(n_blocks, block_size)
    me = lax.axis_index("gx")
    slab = jnp.zeros((devices, 8, 128), jnp.float32)
    slab = lax.dynamic_update_slice(slab, jnp.zeros((1, 8, 128), jnp.float32).at[0, 0, : chan_map.shape[0]].set(chan_map.astype(jnp.float32)), (me, 0, 0))
    all_chan = lax.psum(slab, "gx")[:, 0, : chan_map.shape[0]].reshape(-1).astype(jnp.int32)
    fresh = [beamform(volt_blocks[i], freq_blocks[i], beam_pos) for i in range(n_blocks)]
    fresh_bins = jnp.concatenate(fresh, axis=0)
    all_chan, fresh_bins = lax.optimization_barrier((all_chan, fresh_bins))
    spectra = spectra_of(history, fresh_bins)
    bins = 2 * spectra.shape[0]
    turned = lax.all_to_all(spectra, "gx", split_axis=0, concat_axis=2, tiled=True)
    freq_dev = turned.shape[0]
    lags = channel_lags(all_chan, channel_count)
    kp1 = lax.axis_index("gx") * freq_dev + jnp.arange(freq_dev, dtype=jnp.int32) + 1
    return dedisperse(kp1, dm_list, lags, turned, bins)


def solution(mesh):
    in_specs = (
        P(("groups", "gx"), None, None, None),
        P(("groups", "gx"), None, None),
        P(),
        P(),
        P("gx"),
    )
    out_specs = P(("groups", "gx"), None, None)
    return jax.shard_map(local, mesh=mesh, in_specs=in_specs, out_specs=out_specs, check_vma=False)
```

```python
from functools import partial
import math

import jax
import jax.numpy as jnp
from jax import lax
from jax.experimental import pallas as pl
from jax.experimental.pallas import tpu as pltpu
from jax.sharding import PartitionSpec as P

GRID = 32
PHASES = 8192


def axis_tables(nu, pos, scale):
    step = (nu[:, None] * pos[None, :]) % PHASES

    def trig(mult, factor):
        turns = (step[:, None, :] * (mult[None, :, None] * factor)) % PHASES
        angles = turns.astype(jnp.float32) * (2.0 * math.pi / PHASES)
        return jnp.cos(angles), jnp.sin(angles)

    lo = jnp.arange(8, dtype=jnp.int32)
    hi = jnp.arange(GRID // 8, dtype=jnp.int32)
    c_lo, s_lo = trig(lo, 1)
    c_hi, s_hi = trig(hi, 8)
    cos_t = c_hi[:, :, None, :] * c_lo[:, None, :, :] - s_hi[:, :, None, :] * s_lo[:, None, :, :]
    sin_t = s_hi[:, :, None, :] * c_lo[:, None, :, :] + c_hi[:, :, None, :] * s_lo[:, None, :, :]
    shape = (nu.shape[0], GRID, pos.shape[0])
    return cos_t.reshape(shape) * scale, sin_t.reshape(shape) * scale


def steering(nu, beam_pos, antennas):
    weight_scale = 1.0 / math.sqrt(antennas)
    ca, sa = axis_tables(nu, beam_pos[:, 0], weight_scale)
    cb, sb = axis_tables(nu, beam_pos[:, 1], 1.0)
    n_chan, _, beams = ca.shape
    w_cos = ca[:, None, :, :] * cb[:, :, None, :] - sa[:, None, :, :] * sb[:, :, None, :]
    w_sin = sa[:, None, :, :] * cb[:, :, None, :] + ca[:, None, :, :] * sb[:, :, None, :]
    w_cos = w_cos.reshape(n_chan, GRID * GRID, beams).astype(jnp.bfloat16)
    w_sin = w_sin.reshape(n_chan, GRID * GRID, beams).astype(jnp.bfloat16)
    return w_cos, w_sin


def dft_table(bins):
    sample = jnp.arange(bins, dtype=jnp.int32)
    harmonic = jnp.arange(bins // 2, dtype=jnp.int32) + 1
    turn_count = sample[:, None] * harmonic[None, :] % bins
    angles = turn_count.astype(jnp.float32) * (2.0 * math.pi / bins)
    norm_scale = 1.0 / math.sqrt(bins)
    both = jnp.stack([jnp.cos(angles) * norm_scale, -jnp.sin(angles) * norm_scale], axis=2)
    return both.reshape(bins, bins)


def channel_lags(chan_map, channel_count):
    freq_index = 2 * channel_count - chan_map
    top_square = 2 * channel_count * (2 * channel_count) * 64
    return top_square // (freq_index * freq_index) - 64


def dedisp_kernel(resid_ref, tab_ref, spec_ref, out_ref, lhs_buf, rhs_buf, *, channels):
    rows = resid_ref.shape[0]
    cos_t = jnp.broadcast_to(tab_ref[0, 0:1, :], (rows, 128))
    sin_t = jnp.broadcast_to(tab_ref[0, 1:2, :], (rows, 128))
    for c in range(channels // 128):
        idx = resid_ref[:, c * 128:(c + 1) * 128]
        lhs_buf[:, c * 128:(c + 1) * 128] = jnp.take_along_axis(cos_t, idx, axis=1).astype(jnp.bfloat16)
        lhs_buf[:, channels + c * 128:channels + (c + 1) * 128] = (
            jnp.take_along_axis(sin_t, idx, axis=1).astype(jnp.bfloat16)
        )
    sources, _, _, chans, beams = spec_ref.shape
    for s in range(sources):
        s_re = spec_ref[s, 0, 0]
        s_im = spec_ref[s, 0, 1]
        lo, hi = s * chans, (s + 1) * chans
        rhs_buf[lo:hi, 0:beams] = s_re
        rhs_buf[lo:hi, beams:2 * beams] = s_im
        rhs_buf[channels + lo:channels + hi, 0:beams] = -s_im
        rhs_buf[channels + lo:channels + hi, beams:2 * beams] = s_re
    res = jnp.dot(lhs_buf[...], rhs_buf[...], preferred_element_type=jnp.float32)
    ded_re = res[:, 0:beams]
    ded_im = res[:, beams:2 * beams]
    out_ref[0] = (ded_re * ded_re + ded_im * ded_im) / channels


def dedisperse(kp1, dm_list, lags, spec, bins):
    sources, n_freq, _, chans, beams = spec.shape
    channels = sources * chans
    trials = dm_list.shape[0]
    resid = ((dm_list[:, None] * lags[None, :]) // 4096) % bins
    sample = jnp.arange(128, dtype=jnp.int32) % bins
    turns = (kp1[:, None] * sample[None, :]) % bins
    angles = turns.astype(jnp.float32) * (2.0 * math.pi / bins)
    tab = jnp.zeros((n_freq, 8, 128), jnp.float32)
    tab = tab.at[:, 0].set(jnp.cos(angles).astype(jnp.bfloat16).astype(jnp.float32))
    tab = tab.at[:, 1].set(jnp.sin(angles).astype(jnp.bfloat16).astype(jnp.float32))
    flops = 8 * n_freq * trials * channels * beams
    cost = pl.CostEstimate(
        flops=flops,
        transcendentals=0,
        bytes_accessed=trials * channels * 4 + n_freq * 2 * channels * beams * 2 + n_freq * trials * beams * 4,
    )
    return pl.pallas_call(
        partial(dedisp_kernel, channels=channels),
        out_shape=jax.ShapeDtypeStruct((n_freq, trials, beams), jnp.float32),
        grid=(n_freq,),
        in_specs=[
            pl.BlockSpec((trials, channels), lambda i: (0, 0)),
            pl.BlockSpec((1, 8, 128), lambda i: (i, 0, 0)),
            pl.BlockSpec((sources, 1, 2, chans, beams), lambda i: (0, i, 0, 0, 0)),
        ],
        out_specs=pl.BlockSpec((1, trials, beams), lambda i: (i, 0, 0)),
        scratch_shapes=[
            pltpu.VMEM((trials, 2 * channels), jnp.bfloat16),
            pltpu.VMEM((2 * channels, 2 * beams), jnp.bfloat16),
        ],
        compiler_params=pltpu.CompilerParams(vmem_limit_bytes=48 * 1024 * 1024),
        cost_estimate=cost,
    )(resid, tab, spec)


def beamform(volt_block, nu, beam_pos):
    n_chan, _, samples, antennas = volt_block.shape
    beams = beam_pos.shape[0]
    cos_w, sin_w = steering(nu, beam_pos, antennas)
    cosine_term = jnp.einsum("cpsa,cab->cpsb", volt_block, cos_w, preferred_element_type=jnp.float32)
    sin_part = jnp.einsum("cpsa,cab->cpsb", volt_block, sin_w, preferred_element_type=jnp.float32)
    real_part = cosine_term[:, 0] + sin_part[:, 1]
    imag_part = cosine_term[:, 1] - sin_part[:, 0]
    power_now = real_part * real_part + imag_part * imag_part
    return jnp.mean(power_now.reshape(n_chan, samples // 4, 4, beams), axis=2)


def spectra_of(history, fresh_bins):
    highest = lax.Precision.HIGHEST
    window = jnp.concatenate([history, fresh_bins], axis=1)
    bins = window.shape[1]
    scaled = window / (jnp.mean(window, axis=1, keepdims=True) + 1e-06)
    spectra = jnp.einsum("ctb,tj->jcb", scaled, dft_table(bins), precision=highest).astype(jnp.bfloat16)
    return spectra.reshape(bins // 2, 2, history.shape[0], history.shape[2])


def local(voltages, history, beam_pos, dm_list, chan_map):
    devices = lax.axis_size("gx")
    channel_count = devices * chan_map.shape[0]
    local_chan = voltages.shape[0]
    block_size = math.gcd(local_chan, 8)
    n_blocks = local_chan // block_size
    volt_blocks = voltages.reshape(n_blocks, block_size, *voltages.shape[1:])
    freq_blocks = (2 * channel_count - chan_map).reshape(n_blocks, block_size)
    all_chan = lax.all_gather(chan_map, "gx", axis=0, tiled=True)
    all_chan, volt_blocks = lax.optimization_barrier((all_chan, volt_blocks))
    fresh = [beamform(volt_blocks[i], freq_blocks[i], beam_pos) for i in range(n_blocks)]
    fresh_bins = jnp.concatenate(fresh, axis=0)
    spectra = spectra_of(history, fresh_bins)
    bins = 2 * spectra.shape[0]
    freq_dev = spectra.shape[0] // devices
    blocks = spectra.reshape(devices, freq_dev, *spectra.shape[1:])
    turned = lax.all_to_all(blocks, "gx", split_axis=0, concat_axis=0, tiled=True)
    lags = channel_lags(all_chan, channel_count)
    kp1 = lax.axis_index("gx") * freq_dev + jnp.arange(freq_dev, dtype=jnp.int32) + 1
    return dedisperse(kp1, dm_list, lags, turned, bins)


def solution(mesh):
    in_specs = (
        P(("groups", "gx"), None, None, None),
        P(("groups", "gx"), None, None),
        P(),
        P(),
        P("gx"),
    )
    out_specs = P(("groups", "gx"), None, None)
    return jax.shard_map(local, mesh=mesh, in_specs=in_specs, out_specs=out_specs, check_vma=False)
```

```python
from functools import partial
import math

import jax
import jax.numpy as jnp
from jax import lax
from jax.experimental import pallas as pl
from jax.experimental.pallas import tpu as pltpu
from jax.sharding import PartitionSpec as P

GRID = 32
PHASES = 8192


def axis_tables(nu, pos, scale):
    step = (nu[:, None] * pos[None, :]) % PHASES

    def trig(mult, factor):
        turns = (step[:, None, :] * (mult[None, :, None] * factor)) % PHASES
        angles = turns.astype(jnp.float32) * (2.0 * math.pi / PHASES)
        return jnp.cos(angles), jnp.sin(angles)

    lo = jnp.arange(8, dtype=jnp.int32)
    hi = jnp.arange(GRID // 8, dtype=jnp.int32)
    c_lo, s_lo = trig(lo, 1)
    c_hi, s_hi = trig(hi, 8)
    cos_t = c_hi[:, :, None, :] * c_lo[:, None, :, :] - s_hi[:, :, None, :] * s_lo[:, None, :, :]
    sin_t = s_hi[:, :, None, :] * c_lo[:, None, :, :] + c_hi[:, :, None, :] * s_lo[:, None, :, :]
    shape = (nu.shape[0], GRID, pos.shape[0])
    return cos_t.reshape(shape) * scale, sin_t.reshape(shape) * scale


def steering(nu, beam_pos, antennas):
    weight_scale = 1.0 / math.sqrt(antennas)
    ca, sa = axis_tables(nu, beam_pos[:, 0], weight_scale)
    cb, sb = axis_tables(nu, beam_pos[:, 1], 1.0)
    n_chan, _, beams = ca.shape
    w_cos = ca[:, None, :, :] * cb[:, :, None, :] - sa[:, None, :, :] * sb[:, :, None, :]
    w_sin = sa[:, None, :, :] * cb[:, :, None, :] + ca[:, None, :, :] * sb[:, :, None, :]
    return w_cos.astype(jnp.bfloat16), w_sin.astype(jnp.bfloat16)


def dft_table(bins):
    sample = jnp.arange(bins, dtype=jnp.int32)
    harmonic = jnp.arange(bins // 2, dtype=jnp.int32) + 1
    turn_count = sample[:, None] * harmonic[None, :] % bins
    angles = turn_count.astype(jnp.float32) * (2.0 * math.pi / bins)
    norm_scale = 1.0 / math.sqrt(bins)
    both = jnp.stack([jnp.cos(angles) * norm_scale, -jnp.sin(angles) * norm_scale], axis=2)
    return both.reshape(bins, bins)


def channel_lags(chan_map, channel_count):
    freq_index = 2 * channel_count - chan_map
    top_square = 2 * channel_count * (2 * channel_count) * 64
    return top_square // (freq_index * freq_index) - 64


def dedisp_kernel(resid_ref, tab_ref, spec_ref, out_ref, lhs_buf, rhs_buf, *, channels):
    rows = resid_ref.shape[0]
    cos_t = jnp.broadcast_to(tab_ref[0, 0:1, :], (rows, 128))
    sin_t = jnp.broadcast_to(tab_ref[0, 1:2, :], (rows, 128))
    for c in range(channels // 128):
        idx = resid_ref[:, c * 128:(c + 1) * 128]
        lhs_buf[:, c * 128:(c + 1) * 128] = jnp.take_along_axis(cos_t, idx, axis=1).astype(jnp.bfloat16)
        lhs_buf[:, channels + c * 128:channels + (c + 1) * 128] = (
            jnp.take_along_axis(sin_t, idx, axis=1).astype(jnp.bfloat16)
        )
    sources, _, _, chans, beams = spec_ref.shape
    for s in range(sources):
        s_re = spec_ref[s, 0, 0]
        s_im = spec_ref[s, 0, 1]
        lo, hi = s * chans, (s + 1) * chans
        rhs_buf[lo:hi, 0:beams] = s_re
        rhs_buf[lo:hi, beams:2 * beams] = s_im
        rhs_buf[channels + lo:channels + hi, 0:beams] = -s_im
        rhs_buf[channels + lo:channels + hi, beams:2 * beams] = s_re
    res = jnp.dot(lhs_buf[...], rhs_buf[...], preferred_element_type=jnp.float32)
    ded_re = res[:, 0:beams]
    ded_im = res[:, beams:2 * beams]
    out_ref[0] = (ded_re * ded_re + ded_im * ded_im) / channels


def dedisperse(kp1, dm_list, lags, spec, bins):
    sources, n_freq, _, chans, beams = spec.shape
    channels = sources * chans
    trials = dm_list.shape[0]
    resid = ((dm_list[:, None] * lags[None, :]) // 4096) % bins
    sample = jnp.arange(128, dtype=jnp.int32) % bins
    turns = (kp1[:, None] * sample[None, :]) % bins
    angles = turns.astype(jnp.float32) * (2.0 * math.pi / bins)
    tab = jnp.zeros((n_freq, 8, 128), jnp.float32)
    tab = tab.at[:, 0].set(jnp.cos(angles).astype(jnp.bfloat16).astype(jnp.float32))
    tab = tab.at[:, 1].set(jnp.sin(angles).astype(jnp.bfloat16).astype(jnp.float32))
    flops = 8 * n_freq * trials * channels * beams
    cost = pl.CostEstimate(
        flops=flops,
        transcendentals=0,
        bytes_accessed=trials * channels * 4 + n_freq * 2 * channels * beams * 2 + n_freq * trials * beams * 4,
    )
    return pl.pallas_call(
        partial(dedisp_kernel, channels=channels),
        out_shape=jax.ShapeDtypeStruct((n_freq, trials, beams), jnp.float32),
        grid=(n_freq,),
        in_specs=[
            pl.BlockSpec((trials, channels), lambda i: (0, 0)),
            pl.BlockSpec((1, 8, 128), lambda i: (i, 0, 0)),
            pl.BlockSpec((sources, 1, 2, chans, beams), lambda i: (0, i, 0, 0, 0)),
        ],
        out_specs=pl.BlockSpec((1, trials, beams), lambda i: (i, 0, 0)),
        scratch_shapes=[
            pltpu.VMEM((trials, 2 * channels), jnp.bfloat16),
            pltpu.VMEM((2 * channels, 2 * beams), jnp.bfloat16),
        ],
        compiler_params=pltpu.CompilerParams(vmem_limit_bytes=48 * 1024 * 1024),
        cost_estimate=cost,
    )(resid, tab, spec)


def beamform(volt_block, nu, beam_pos):
    n_chan, _, samples, antennas = volt_block.shape
    beams = beam_pos.shape[0]
    cos_w, sin_w = steering(nu, beam_pos, antennas)
    volt_grid = volt_block.reshape(n_chan, 2, samples, GRID, antennas // GRID)
    cosine_term = jnp.einsum("cpsne,cneb->cpsb", volt_grid, cos_w, preferred_element_type=jnp.float32)
    sin_part = jnp.einsum("cpsne,cneb->cpsb", volt_grid, sin_w, preferred_element_type=jnp.float32)
    real_part = cosine_term[:, 0] + sin_part[:, 1]
    imag_part = cosine_term[:, 1] - sin_part[:, 0]
    power_now = real_part * real_part + imag_part * imag_part
    return jnp.mean(power_now.reshape(n_chan, samples // 4, 4, beams), axis=2)


def spectra_of(history, fresh_bins):
    highest = lax.Precision.HIGHEST
    window = jnp.concatenate([history, fresh_bins], axis=1)
    bins = window.shape[1]
    scaled = window / (jnp.mean(window, axis=1, keepdims=True) + 1e-06)
    spectra = jnp.einsum("ctb,tj->jcb", scaled, dft_table(bins), precision=highest).astype(jnp.bfloat16)
    return spectra.reshape(bins // 2, 2, history.shape[0], history.shape[2])


def local(voltages, history, beam_pos, dm_list, chan_map):
    devices = lax.axis_size("gx")
    channel_count = devices * chan_map.shape[0]
    local_chan = voltages.shape[0]
    block_size = math.gcd(local_chan, 8)
    n_blocks = local_chan // block_size
    volt_blocks = voltages.reshape(n_blocks, block_size, *voltages.shape[1:])
    freq_blocks = (2 * channel_count - chan_map).reshape(n_blocks, block_size)
    all_chan = lax.all_gather(chan_map, "gx", axis=0, tiled=True)
    all_chan, volt_blocks = lax.optimization_barrier((all_chan, volt_blocks))
    fresh = [beamform(volt_blocks[i], freq_blocks[i], beam_pos) for i in range(n_blocks)]
    fresh_bins = jnp.concatenate(fresh, axis=0)
    spectra = spectra_of(history, fresh_bins)
    bins = 2 * spectra.shape[0]
    freq_dev = spectra.shape[0] // devices
    blocks = spectra.reshape(devices, freq_dev, *spectra.shape[1:])
    turned = lax.all_to_all(blocks, "gx", split_axis=0, concat_axis=0, tiled=True)
    lags = channel_lags(all_chan, channel_count)
    kp1 = lax.axis_index("gx") * freq_dev + jnp.arange(freq_dev, dtype=jnp.int32) + 1
    return dedisperse(kp1, dm_list, lags, turned, bins)


def solution(mesh):
    in_specs = (
        P(("groups", "gx"), None, None, None),
        P(("groups", "gx"), None, None),
        P(),
        P(),
        P("gx"),
    )
    out_specs = P(("groups", "gx"), None, None)
    return jax.shard_map(local, mesh=mesh, in_specs=in_specs, out_specs=out_specs, check_vma=False)
```

```python
from functools import partial
import math

import jax
import jax.numpy as jnp
from jax import lax
from jax.experimental import pallas as pl
from jax.experimental.pallas import tpu as pltpu
from jax.sharding import PartitionSpec as P

GRID = 32
PHASES = 8192


def axis_tables(nu, pos, scale):
    step = (nu[:, None] * pos[None, :]) % PHASES

    def trig(mult, factor):
        turns = (step[:, None, :] * (mult[None, :, None] * factor)) % PHASES
        angles = turns.astype(jnp.float32) * (2.0 * math.pi / PHASES)
        return jnp.cos(angles), jnp.sin(angles)

    lo = jnp.arange(8, dtype=jnp.int32)
    hi = jnp.arange(GRID // 8, dtype=jnp.int32)
    c_lo, s_lo = trig(lo, 1)
    c_hi, s_hi = trig(hi, 8)
    cos_t = c_hi[:, :, None, :] * c_lo[:, None, :, :] - s_hi[:, :, None, :] * s_lo[:, None, :, :]
    sin_t = s_hi[:, :, None, :] * c_lo[:, None, :, :] + c_hi[:, :, None, :] * s_lo[:, None, :, :]
    shape = (nu.shape[0], GRID, pos.shape[0])
    return cos_t.reshape(shape) * scale, sin_t.reshape(shape) * scale


def steering(nu, beam_pos, antennas):
    weight_scale = 1.0 / math.sqrt(antennas)
    ca, sa = axis_tables(nu, beam_pos[:, 0], weight_scale)
    cb, sb = axis_tables(nu, beam_pos[:, 1], 1.0)
    n_chan, _, beams = ca.shape
    w_cos = ca[:, None, :, :] * cb[:, :, None, :] - sa[:, None, :, :] * sb[:, :, None, :]
    w_sin = sa[:, None, :, :] * cb[:, :, None, :] + ca[:, None, :, :] * sb[:, :, None, :]
    w_cos = w_cos.reshape(n_chan, GRID * GRID, beams).astype(jnp.bfloat16)
    w_sin = w_sin.reshape(n_chan, GRID * GRID, beams).astype(jnp.bfloat16)
    return w_cos, w_sin


def dft_table(bins):
    sample = jnp.arange(bins, dtype=jnp.int32)
    harmonic = jnp.arange(bins // 2, dtype=jnp.int32) + 1
    turn_count = sample[:, None] * harmonic[None, :] % bins
    angles = turn_count.astype(jnp.float32) * (2.0 * math.pi / bins)
    norm_scale = 1.0 / math.sqrt(bins)
    both = jnp.stack([jnp.cos(angles) * norm_scale, -jnp.sin(angles) * norm_scale], axis=2)
    return both.reshape(bins, bins)


def channel_lags(chan_map, channel_count):
    freq_index = 2 * channel_count - chan_map
    top_square = 2 * channel_count * (2 * channel_count) * 64
    return top_square // (freq_index * freq_index) - 64


def dedisp_kernel(resid_ref, tab_ref, spec_ref, out_ref, lhs_buf, rhs_buf, *, channels):
    sources, _, _, chans, beams = spec_ref.shape
    for s in range(sources):
        s_re = spec_ref[s, 0, 0]
        s_im = spec_ref[s, 0, 1]
        lo, hi = s * chans, (s + 1) * chans
        rhs_buf[lo:hi, 0:beams] = s_re
        rhs_buf[lo:hi, beams:2 * beams] = s_im
        rhs_buf[channels + lo:channels + hi, 0:beams] = -s_im
        rhs_buf[channels + lo:channels + hi, beams:2 * beams] = s_re
    rows = resid_ref.shape[0]
    step = 256 if rows % 256 == 0 else rows
    cos_t = jnp.broadcast_to(tab_ref[0, 0:1, :], (step, 128))
    sin_t = jnp.broadcast_to(tab_ref[0, 1:2, :], (step, 128))
    for r in range(rows // step):
        band = slice(r * step, (r + 1) * step)
        for c in range(channels // 128):
            idx = resid_ref[band, c * 128:(c + 1) * 128]
            lhs_buf[band, c * 128:(c + 1) * 128] = jnp.take_along_axis(cos_t, idx, axis=1).astype(jnp.bfloat16)
            lhs_buf[band, channels + c * 128:channels + (c + 1) * 128] = (
                jnp.take_along_axis(sin_t, idx, axis=1).astype(jnp.bfloat16)
            )
        res = jnp.dot(lhs_buf[band, :], rhs_buf[...], preferred_element_type=jnp.float32)
        ded_re = res[:, 0:beams]
        ded_im = res[:, beams:2 * beams]
        out_ref[0, band, :] = (ded_re * ded_re + ded_im * ded_im) / channels


def dedisperse(kp1, dm_list, lags, spec, bins):
    sources, n_freq, _, chans, beams = spec.shape
    channels = sources * chans
    trials = dm_list.shape[0]
    resid = ((dm_list[:, None] * lags[None, :]) // 4096) % bins
    sample = jnp.arange(128, dtype=jnp.int32) % bins
    turns = (kp1[:, None] * sample[None, :]) % bins
    angles = turns.astype(jnp.float32) * (2.0 * math.pi / bins)
    tab = jnp.zeros((n_freq, 8, 128), jnp.float32)
    tab = tab.at[:, 0].set(jnp.cos(angles).astype(jnp.bfloat16).astype(jnp.float32))
    tab = tab.at[:, 1].set(jnp.sin(angles).astype(jnp.bfloat16).astype(jnp.float32))
    flops = 8 * n_freq * trials * channels * beams
    cost = pl.CostEstimate(
        flops=flops,
        transcendentals=0,
        bytes_accessed=trials * channels * 4 + n_freq * 2 * channels * beams * 2 + n_freq * trials * beams * 4,
    )
    return pl.pallas_call(
        partial(dedisp_kernel, channels=channels),
        out_shape=jax.ShapeDtypeStruct((n_freq, trials, beams), jnp.float32),
        grid=(n_freq,),
        in_specs=[
            pl.BlockSpec((trials, channels), lambda i: (0, 0)),
            pl.BlockSpec((1, 8, 128), lambda i: (i, 0, 0)),
            pl.BlockSpec((sources, 1, 2, chans, beams), lambda i: (0, i, 0, 0, 0)),
        ],
        out_specs=pl.BlockSpec((1, trials, beams), lambda i: (i, 0, 0)),
        scratch_shapes=[
            pltpu.VMEM((trials, 2 * channels), jnp.bfloat16),
            pltpu.VMEM((2 * channels, 2 * beams), jnp.bfloat16),
        ],
        compiler_params=pltpu.CompilerParams(vmem_limit_bytes=48 * 1024 * 1024),
        cost_estimate=cost,
    )(resid, tab, spec)


def beamform(volt_block, nu, beam_pos):
    n_chan, _, samples, antennas = volt_block.shape
    beams = beam_pos.shape[0]
    cos_w, sin_w = steering(nu, beam_pos, antennas)
    cosine_term = jnp.einsum("cpsa,cab->cpsb", volt_block, cos_w, preferred_element_type=jnp.float32)
    sin_part = jnp.einsum("cpsa,cab->cpsb", volt_block, sin_w, preferred_element_type=jnp.float32)
    real_part = cosine_term[:, 0] + sin_part[:, 1]
    imag_part = cosine_term[:, 1] - sin_part[:, 0]
    power_now = real_part * real_part + imag_part * imag_part
    return jnp.mean(power_now.reshape(n_chan, samples // 4, 4, beams), axis=2)


def spectra_of(history, fresh_bins):
    highest = lax.Precision.HIGHEST
    window = jnp.concatenate([history, fresh_bins], axis=1)
    bins = window.shape[1]
    scaled = window / (jnp.mean(window, axis=1, keepdims=True) + 1e-06)
    spectra = jnp.einsum("ctb,tj->jcb", scaled, dft_table(bins), precision=highest).astype(jnp.bfloat16)
    return spectra.reshape(bins // 2, 2, history.shape[0], history.shape[2])


def local(voltages, history, beam_pos, dm_list, chan_map):
    devices = lax.axis_size("gx")
    channel_count = devices * chan_map.shape[0]
    local_chan = voltages.shape[0]
    block_size = math.gcd(local_chan, 8)
    n_blocks = local_chan // block_size
    volt_blocks = voltages.reshape(n_blocks, block_size, *voltages.shape[1:])
    freq_blocks = (2 * channel_count - chan_map).reshape(n_blocks, block_size)
    all_chan = lax.all_gather(chan_map, "gx", axis=0, tiled=True)
    all_chan, volt_blocks = lax.optimization_barrier((all_chan, volt_blocks))
    fresh = [beamform(volt_blocks[i], freq_blocks[i], beam_pos) for i in range(n_blocks)]
    fresh_bins = jnp.concatenate(fresh, axis=0)
    spectra = spectra_of(history, fresh_bins)
    bins = 2 * spectra.shape[0]
    freq_dev = spectra.shape[0] // devices
    blocks = spectra.reshape(devices, freq_dev, *spectra.shape[1:])
    turned = lax.all_to_all(blocks, "gx", split_axis=0, concat_axis=0, tiled=True)
    lags = channel_lags(all_chan, channel_count)
    kp1 = lax.axis_index("gx") * freq_dev + jnp.arange(freq_dev, dtype=jnp.int32) + 1
    return dedisperse(kp1, dm_list, lags, turned, bins)


def solution(mesh):
    in_specs = (
        P(("groups", "gx"), None, None, None),
        P(("groups", "gx"), None, None),
        P(),
        P(),
        P("gx"),
    )
    out_specs = P(("groups", "gx"), None, None)
    return jax.shard_map(local, mesh=mesh, in_specs=in_specs, out_specs=out_specs, check_vma=False)
```

```python
from functools import partial
import math

import jax
import jax.numpy as jnp
from jax import lax
from jax.experimental import pallas as pl
from jax.experimental.pallas import tpu as pltpu
from jax.sharding import PartitionSpec as P

GRID = 32
PHASES = 8192


def axis_tables(nu, pos, scale):
    step = (nu[:, None] * pos[None, :]) % PHASES

    def trig(mult, factor):
        turns = (step[:, None, :] * (mult[None, :, None] * factor)) % PHASES
        angles = turns.astype(jnp.float32) * (2.0 * math.pi / PHASES)
        return jnp.cos(angles), jnp.sin(angles)

    lo = jnp.arange(8, dtype=jnp.int32)
    hi = jnp.arange(GRID // 8, dtype=jnp.int32)
    c_lo, s_lo = trig(lo, 1)
    c_hi, s_hi = trig(hi, 8)
    cos_t = c_hi[:, :, None, :] * c_lo[:, None, :, :] - s_hi[:, :, None, :] * s_lo[:, None, :, :]
    sin_t = s_hi[:, :, None, :] * c_lo[:, None, :, :] + c_hi[:, :, None, :] * s_lo[:, None, :, :]
    shape = (nu.shape[0], GRID, pos.shape[0])
    return cos_t.reshape(shape) * scale, sin_t.reshape(shape) * scale


def steering(nu, beam_pos, antennas):
    weight_scale = 1.0 / math.sqrt(antennas)
    ca, sa = axis_tables(nu, beam_pos[:, 0], weight_scale)
    cb, sb = axis_tables(nu, beam_pos[:, 1], 1.0)
    n_chan, _, beams = ca.shape
    w_cos = ca[:, None, :, :] * cb[:, :, None, :] - sa[:, None, :, :] * sb[:, :, None, :]
    w_sin = sa[:, None, :, :] * cb[:, :, None, :] + ca[:, None, :, :] * sb[:, :, None, :]
    w_cos = w_cos.reshape(n_chan, GRID * GRID, beams).astype(jnp.bfloat16)
    w_sin = w_sin.reshape(n_chan, GRID * GRID, beams).astype(jnp.bfloat16)
    return w_cos, w_sin


def dft_table(bins):
    sample = jnp.arange(bins, dtype=jnp.int32)
    harmonic = jnp.arange(bins // 2, dtype=jnp.int32) + 1
    turn_count = sample[:, None] * harmonic[None, :] % bins
    angles = turn_count.astype(jnp.float32) * (2.0 * math.pi / bins)
    norm_scale = 1.0 / math.sqrt(bins)
    both = jnp.stack([jnp.cos(angles) * norm_scale, -jnp.sin(angles) * norm_scale], axis=2)
    return both.reshape(bins, bins)


def channel_lags(chan_map, channel_count):
    freq_index = 2 * channel_count - chan_map
    top_square = 2 * channel_count * (2 * channel_count) * 64
    return top_square // (freq_index * freq_index) - 64


def dedisp_kernel(resid_ref, tab_ref, spec_ref, out_ref, lhs_buf, rhs_buf, *, channels):
    sources, _, _, chans, beams = spec_ref.shape
    for s in range(sources):
        s_re = spec_ref[s, 0, 0]
        s_im = spec_ref[s, 0, 1]
        lo, hi = s * chans, (s + 1) * chans
        rhs_buf[lo:hi, 0:beams] = s_re
        rhs_buf[lo:hi, beams:2 * beams] = s_im
        rhs_buf[channels + lo:channels + hi, 0:beams] = -s_im
        rhs_buf[channels + lo:channels + hi, beams:2 * beams] = s_re
    rows = resid_ref.shape[0]
    step = 128 if rows % 128 == 0 else rows
    cos_t = jnp.broadcast_to(tab_ref[0, 0:1, :], (step, 128))
    sin_t = jnp.broadcast_to(tab_ref[0, 1:2, :], (step, 128))
    for r in range(rows // step):
        band = slice(r * step, (r + 1) * step)
        for c in range(channels // 128):
            idx = resid_ref[band, c * 128:(c + 1) * 128]
            lhs_buf[band, c * 128:(c + 1) * 128] = jnp.take_along_axis(cos_t, idx, axis=1).astype(jnp.bfloat16)
            lhs_buf[band, channels + c * 128:channels + (c + 1) * 128] = (
                jnp.take_along_axis(sin_t, idx, axis=1).astype(jnp.bfloat16)
            )
        res = jnp.dot(lhs_buf[band, :], rhs_buf[...], preferred_element_type=jnp.float32)
        ded_re = res[:, 0:beams]
        ded_im = res[:, beams:2 * beams]
        out_ref[0, band, :] = (ded_re * ded_re + ded_im * ded_im) / channels


def dedisperse(kp1, dm_list, lags, spec, bins):
    sources, n_freq, _, chans, beams = spec.shape
    channels = sources * chans
    trials = dm_list.shape[0]
    resid = ((dm_list[:, None] * lags[None, :]) // 4096) % bins
    sample = jnp.arange(128, dtype=jnp.int32) % bins
    turns = (kp1[:, None] * sample[None, :]) % bins
    angles = turns.astype(jnp.float32) * (2.0 * math.pi / bins)
    tab = jnp.zeros((n_freq, 8, 128), jnp.float32)
    tab = tab.at[:, 0].set(jnp.cos(angles).astype(jnp.bfloat16).astype(jnp.float32))
    tab = tab.at[:, 1].set(jnp.sin(angles).astype(jnp.bfloat16).astype(jnp.float32))
    flops = 8 * n_freq * trials * channels * beams
    cost = pl.CostEstimate(
        flops=flops,
        transcendentals=0,
        bytes_accessed=trials * channels * 4 + n_freq * 2 * channels * beams * 2 + n_freq * trials * beams * 4,
    )
    return pl.pallas_call(
        partial(dedisp_kernel, channels=channels),
        out_shape=jax.ShapeDtypeStruct((n_freq, trials, beams), jnp.float32),
        grid=(n_freq,),
        in_specs=[
            pl.BlockSpec((trials, channels), lambda i: (0, 0)),
            pl.BlockSpec((1, 8, 128), lambda i: (i, 0, 0)),
            pl.BlockSpec((sources, 1, 2, chans, beams), lambda i: (0, i, 0, 0, 0)),
        ],
        out_specs=pl.BlockSpec((1, trials, beams), lambda i: (i, 0, 0)),
        scratch_shapes=[
            pltpu.VMEM((trials, 2 * channels), jnp.bfloat16),
            pltpu.VMEM((2 * channels, 2 * beams), jnp.bfloat16),
        ],
        compiler_params=pltpu.CompilerParams(vmem_limit_bytes=48 * 1024 * 1024),
        cost_estimate=cost,
    )(resid, tab, spec)


def beamform(volt_block, nu, beam_pos):
    n_chan, _, samples, antennas = volt_block.shape
    beams = beam_pos.shape[0]
    cos_w, sin_w = steering(nu, beam_pos, antennas)
    cosine_term = jnp.einsum("cpsa,cab->cpsb", volt_block, cos_w, preferred_element_type=jnp.float32)
    sin_part = jnp.einsum("cpsa,cab->cpsb", volt_block, sin_w, preferred_element_type=jnp.float32)
    real_part = cosine_term[:, 0] + sin_part[:, 1]
    imag_part = cosine_term[:, 1] - sin_part[:, 0]
    power_now = real_part * real_part + imag_part * imag_part
    return jnp.mean(power_now.reshape(n_chan, samples // 4, 4, beams), axis=2)


def spectra_of(history, fresh_bins):
    highest = lax.Precision.HIGHEST
    window = jnp.concatenate([history, fresh_bins], axis=1)
    bins = window.shape[1]
    scaled = window / (jnp.mean(window, axis=1, keepdims=True) + 1e-06)
    spectra = jnp.einsum("ctb,tj->jcb", scaled, dft_table(bins), precision=highest).astype(jnp.bfloat16)
    return spectra.reshape(bins // 2, 2, history.shape[0], history.shape[2])


def local(voltages, history, beam_pos, dm_list, chan_map):
    devices = lax.axis_size("gx")
    channel_count = devices * chan_map.shape[0]
    local_chan = voltages.shape[0]
    block_size = math.gcd(local_chan, 8)
    n_blocks = local_chan // block_size
    volt_blocks = voltages.reshape(n_blocks, block_size, *voltages.shape[1:])
    freq_blocks = (2 * channel_count - chan_map).reshape(n_blocks, block_size)
    all_chan = lax.all_gather(chan_map, "gx", axis=0, tiled=True)
    all_chan, volt_blocks = lax.optimization_barrier((all_chan, volt_blocks))
    fresh = [beamform(volt_blocks[i], freq_blocks[i], beam_pos) for i in range(n_blocks)]
    fresh_bins = jnp.concatenate(fresh, axis=0)
    spectra = spectra_of(history, fresh_bins)
    bins = 2 * spectra.shape[0]
    freq_dev = spectra.shape[0] // devices
    blocks = spectra.reshape(devices, freq_dev, *spectra.shape[1:])
    turned = lax.all_to_all(blocks, "gx", split_axis=0, concat_axis=0, tiled=True)
    lags = channel_lags(all_chan, channel_count)
    kp1 = lax.axis_index("gx") * freq_dev + jnp.arange(freq_dev, dtype=jnp.int32) + 1
    return dedisperse(kp1, dm_list, lags, turned, bins)


def solution(mesh):
    in_specs = (
        P(("groups", "gx"), None, None, None),
        P(("groups", "gx"), None, None),
        P(),
        P(),
        P("gx"),
    )
    out_specs = P(("groups", "gx"), None, None)
    return jax.shard_map(local, mesh=mesh, in_specs=in_specs, out_specs=out_specs, check_vma=False)
```

```python
from functools import partial
import math

import jax
import jax.numpy as jnp
from jax import lax
from jax.experimental import pallas as pl
from jax.experimental.pallas import tpu as pltpu
from jax.sharding import PartitionSpec as P

GRID = 32
PHASES = 8192


def axis_tables(nu, pos, scale):
    step = (nu[:, None] * pos[None, :]) % PHASES

    def trig(mult, factor):
        turns = (step[:, None, :] * (mult[None, :, None] * factor)) % PHASES
        angles = turns.astype(jnp.float32) * (2.0 * math.pi / PHASES)
        return jnp.cos(angles), jnp.sin(angles)

    lo = jnp.arange(8, dtype=jnp.int32)
    hi = jnp.arange(GRID // 8, dtype=jnp.int32)
    c_lo, s_lo = trig(lo, 1)
    c_hi, s_hi = trig(hi, 8)
    cos_t = c_hi[:, :, None, :] * c_lo[:, None, :, :] - s_hi[:, :, None, :] * s_lo[:, None, :, :]
    sin_t = s_hi[:, :, None, :] * c_lo[:, None, :, :] + c_hi[:, :, None, :] * s_lo[:, None, :, :]
    shape = (nu.shape[0], GRID, pos.shape[0])
    return cos_t.reshape(shape) * scale, sin_t.reshape(shape) * scale


def steering(nu, beam_pos, antennas):
    weight_scale = 1.0 / math.sqrt(antennas)
    ca, sa = axis_tables(nu, beam_pos[:, 0], weight_scale)
    cb, sb = axis_tables(nu, beam_pos[:, 1], 1.0)
    n_chan, _, beams = ca.shape
    w_cos = ca[:, None, :, :] * cb[:, :, None, :] - sa[:, None, :, :] * sb[:, :, None, :]
    w_sin = sa[:, None, :, :] * cb[:, :, None, :] + ca[:, None, :, :] * sb[:, :, None, :]
    w_cos = w_cos.reshape(n_chan, GRID * GRID, beams).astype(jnp.bfloat16)
    w_sin = w_sin.reshape(n_chan, GRID * GRID, beams).astype(jnp.bfloat16)
    return w_cos, w_sin


def dft_table(bins):
    sample = jnp.arange(bins, dtype=jnp.int32)
    harmonic = jnp.arange(bins // 2, dtype=jnp.int32) + 1
    turn_count = sample[:, None] * harmonic[None, :] % bins
    angles = turn_count.astype(jnp.float32) * (2.0 * math.pi / bins)
    norm_scale = 1.0 / math.sqrt(bins)
    both = jnp.stack([jnp.cos(angles) * norm_scale, -jnp.sin(angles) * norm_scale], axis=2)
    return both.reshape(bins, bins)


def channel_lags(chan_map, channel_count):
    freq_index = 2 * channel_count - chan_map
    top_square = 2 * channel_count * (2 * channel_count) * 64
    return top_square // (freq_index * freq_index) - 64


def dedisp_kernel(resid_ref, tab_ref, spec_ref, out_ref, lhs_buf, rhs_buf, *, channels):
    sources, _, _, chans, beams = spec_ref.shape
    for s in range(sources):
        s_re = spec_ref[s, 0, 0]
        s_im = spec_ref[s, 0, 1]
        lo, hi = s * chans, (s + 1) * chans
        rhs_buf[lo:hi, 0:beams] = s_re
        rhs_buf[lo:hi, beams:2 * beams] = s_im
        rhs_buf[channels + lo:channels + hi, 0:beams] = -s_im
        rhs_buf[channels + lo:channels + hi, beams:2 * beams] = s_re
    rows = resid_ref.shape[0]
    step = 128 if rows % 128 == 0 else rows
    cos_t = jnp.broadcast_to(tab_ref[0, 0:1, :], (step, 128))
    sin_t = jnp.broadcast_to(tab_ref[0, 1:2, :], (step, 128))
    for r in range(rows // step):
        band = slice(r * step, (r + 1) * step)
        for c in range(channels // 128):
            idx = resid_ref[band, c * 128:(c + 1) * 128]
            lhs_buf[band, c * 128:(c + 1) * 128] = jnp.take_along_axis(cos_t, idx, axis=1).astype(jnp.bfloat16)
            lhs_buf[band, channels + c * 128:channels + (c + 1) * 128] = (
                jnp.take_along_axis(sin_t, idx, axis=1).astype(jnp.bfloat16)
            )
        res = jnp.dot(lhs_buf[band, :], rhs_buf[...], preferred_element_type=jnp.float32)
        ded_re = res[:, 0:beams]
        ded_im = res[:, beams:2 * beams]
        out_ref[0, band, :] = (ded_re * ded_re + ded_im * ded_im) / channels


def dedisperse(kp1, dm_list, lags, spec, bins):
    sources, n_freq, _, chans, beams = spec.shape
    channels = sources * chans
    trials = dm_list.shape[0]
    resid = ((dm_list[:, None] * lags[None, :]) // 4096) % bins
    sample = jnp.arange(128, dtype=jnp.int32) % bins
    turns = (kp1[:, None] * sample[None, :]) % bins
    angles = turns.astype(jnp.float32) * (2.0 * math.pi / bins)
    tab = jnp.zeros((n_freq, 8, 128), jnp.float32)
    tab = tab.at[:, 0].set(jnp.cos(angles).astype(jnp.bfloat16).astype(jnp.float32))
    tab = tab.at[:, 1].set(jnp.sin(angles).astype(jnp.bfloat16).astype(jnp.float32))
    flops = 8 * n_freq * trials * channels * beams
    cost = pl.CostEstimate(
        flops=flops,
        transcendentals=0,
        bytes_accessed=trials * channels * 4 + n_freq * 2 * channels * beams * 2 + n_freq * trials * beams * 4,
    )
    return pl.pallas_call(
        partial(dedisp_kernel, channels=channels),
        out_shape=jax.ShapeDtypeStruct((n_freq, trials, beams), jnp.float32),
        grid=(n_freq,),
        in_specs=[
            pl.BlockSpec((trials, channels), lambda i: (0, 0)),
            pl.BlockSpec((1, 8, 128), lambda i: (i, 0, 0)),
            pl.BlockSpec((sources, 1, 2, chans, beams), lambda i: (0, i, 0, 0, 0)),
        ],
        out_specs=pl.BlockSpec((1, trials, beams), lambda i: (i, 0, 0)),
        scratch_shapes=[
            pltpu.VMEM((trials, 2 * channels), jnp.bfloat16),
            pltpu.VMEM((2 * channels, 2 * beams), jnp.bfloat16),
        ],
        compiler_params=pltpu.CompilerParams(vmem_limit_bytes=48 * 1024 * 1024),
        cost_estimate=cost,
    )(resid, tab, spec)


def beamform(volt_block, nu, beam_pos):
    n_chan, _, samples, antennas = volt_block.shape
    beams = beam_pos.shape[0]
    cos_w, sin_w = steering(nu, beam_pos, antennas)
    cosine_term = jnp.einsum("cpsa,cab->cpsb", volt_block, cos_w, preferred_element_type=jnp.float32)
    sin_part = jnp.einsum("cpsa,cab->cpsb", volt_block, sin_w, preferred_element_type=jnp.float32)
    real_part = cosine_term[:, 0] + sin_part[:, 1]
    imag_part = cosine_term[:, 1] - sin_part[:, 0]
    power_now = real_part * real_part + imag_part * imag_part
    return jnp.mean(power_now.reshape(n_chan, samples // 4, 4, beams), axis=2)


def spectra_of(history, fresh_bins):
    highest = lax.Precision.HIGHEST
    window = jnp.concatenate([history, fresh_bins], axis=1)
    bins = window.shape[1]
    scaled = window / (jnp.mean(window, axis=1, keepdims=True) + 1e-06)
    spectra = jnp.einsum("ctb,tj->jcb", scaled, dft_table(bins), precision=highest).astype(jnp.bfloat16)
    return spectra.reshape(bins // 2, 2, history.shape[0], history.shape[2])


def local(voltages, history, beam_pos, dm_list, chan_map):
    devices = lax.axis_size("gx")
    channel_count = devices * chan_map.shape[0]
    local_chan = voltages.shape[0]
    block_size = math.gcd(local_chan, 8)
    n_blocks = local_chan // block_size
    volt_blocks = voltages.reshape(n_blocks, block_size, *voltages.shape[1:])
    freq_blocks = (2 * channel_count - chan_map).reshape(n_blocks, block_size)
    slot = jnp.arange(channel_count, dtype=jnp.int32) // chan_map.shape[0]
    mine = jnp.where(slot == lax.axis_index("gx"), jnp.tile(chan_map, devices), 0)
    all_chan = lax.psum(mine, "gx")
    all_chan, volt_blocks = lax.optimization_barrier((all_chan, volt_blocks))
    fresh = [beamform(volt_blocks[i], freq_blocks[i], beam_pos) for i in range(n_blocks)]
    fresh_bins = jnp.concatenate(fresh, axis=0)
    spectra = spectra_of(history, fresh_bins)
    bins = 2 * spectra.shape[0]
    freq_dev = spectra.shape[0] // devices
    blocks = spectra.reshape(devices, freq_dev, *spectra.shape[1:])
    turned = lax.all_to_all(blocks, "gx", split_axis=0, concat_axis=0, tiled=True)
    lags = channel_lags(all_chan, channel_count)
    kp1 = lax.axis_index("gx") * freq_dev + jnp.arange(freq_dev, dtype=jnp.int32) + 1
    return dedisperse(kp1, dm_list, lags, turned, bins)


def solution(mesh):
    in_specs = (
        P(("groups", "gx"), None, None, None),
        P(("groups", "gx"), None, None),
        P(),
        P(),
        P("gx"),
    )
    out_specs = P(("groups", "gx"), None, None)
    return jax.shard_map(local, mesh=mesh, in_specs=in_specs, out_specs=out_specs, check_vma=False)
```

```python
from functools import partial
import math

import jax
import jax.numpy as jnp
from jax import lax
from jax.experimental import pallas as pl
from jax.experimental.pallas import tpu as pltpu
from jax.sharding import PartitionSpec as P

GRID = 32
PHASES = 8192


def axis_tables(nu, pos, scale):
    step = (nu[:, None] * pos[None, :]) % PHASES

    def trig(mult, factor):
        turns = (step[:, None, :] * (mult[None, :, None] * factor)) % PHASES
        angles = turns.astype(jnp.float32) * (2.0 * math.pi / PHASES)
        return jnp.cos(angles), jnp.sin(angles)

    lo = jnp.arange(8, dtype=jnp.int32)
    hi = jnp.arange(GRID // 8, dtype=jnp.int32)
    c_lo, s_lo = trig(lo, 1)
    c_hi, s_hi = trig(hi, 8)
    cos_t = c_hi[:, :, None, :] * c_lo[:, None, :, :] - s_hi[:, :, None, :] * s_lo[:, None, :, :]
    sin_t = s_hi[:, :, None, :] * c_lo[:, None, :, :] + c_hi[:, :, None, :] * s_lo[:, None, :, :]
    shape = (nu.shape[0], GRID, pos.shape[0])
    return cos_t.reshape(shape) * scale, sin_t.reshape(shape) * scale


def steering(nu, beam_pos, antennas):
    weight_scale = 1.0 / math.sqrt(antennas)
    ca, sa = axis_tables(nu, beam_pos[:, 0], weight_scale)
    cb, sb = axis_tables(nu, beam_pos[:, 1], 1.0)
    n_chan, _, beams = ca.shape
    w_cos = ca[:, None, :, :] * cb[:, :, None, :] - sa[:, None, :, :] * sb[:, :, None, :]
    w_sin = sa[:, None, :, :] * cb[:, :, None, :] + ca[:, None, :, :] * sb[:, :, None, :]
    w_cos = w_cos.reshape(n_chan, GRID * GRID, beams).astype(jnp.bfloat16)
    w_sin = w_sin.reshape(n_chan, GRID * GRID, beams).astype(jnp.bfloat16)
    return w_cos, w_sin


def dft_table(bins):
    sample = jnp.arange(bins, dtype=jnp.int32)
    harmonic = jnp.arange(bins // 2, dtype=jnp.int32) + 1
    turn_count = sample[:, None] * harmonic[None, :] % bins
    angles = turn_count.astype(jnp.float32) * (2.0 * math.pi / bins)
    norm_scale = 1.0 / math.sqrt(bins)
    both = jnp.stack([jnp.cos(angles) * norm_scale, -jnp.sin(angles) * norm_scale], axis=2)
    return both.reshape(bins, bins)


def channel_lags(chan_map, channel_count):
    freq_index = 2 * channel_count - chan_map
    top_square = 2 * channel_count * (2 * channel_count) * 64
    return top_square // (freq_index * freq_index) - 64


def dedisp_kernel(resid_ref, tab_ref, spec_ref, out_ref, lhs_buf, rhs_buf, *, channels):
    sources, _, _, chans, beams = spec_ref.shape
    for s in range(sources):
        s_re = spec_ref[s, 0, 0]
        s_im = spec_ref[s, 0, 1]
        lo, hi = s * chans, (s + 1) * chans
        rhs_buf[lo:hi, 0:beams] = s_re
        rhs_buf[lo:hi, beams:2 * beams] = s_im
        rhs_buf[channels + lo:channels + hi, 0:beams] = -s_im
        rhs_buf[channels + lo:channels + hi, beams:2 * beams] = s_re
    rows = resid_ref.shape[0]
    step = 128 if rows % 128 == 0 else rows
    cos_t = jnp.broadcast_to(tab_ref[0, 0:1, :], (step, 128))
    sin_t = jnp.broadcast_to(tab_ref[0, 1:2, :], (step, 128))
    for r in range(rows // step):
        band = slice(r * step, (r + 1) * step)
        for c in range(channels // 128):
            idx = resid_ref[band, c * 128:(c + 1) * 128]
            lhs_buf[band, c * 128:(c + 1) * 128] = jnp.take_along_axis(cos_t, idx, axis=1).astype(jnp.bfloat16)
            lhs_buf[band, channels + c * 128:channels + (c + 1) * 128] = (
                jnp.take_along_axis(sin_t, idx, axis=1).astype(jnp.bfloat16)
            )
        res = jnp.dot(lhs_buf[band, :], rhs_buf[...], preferred_element_type=jnp.float32)
        ded_re = res[:, 0:beams]
        ded_im = res[:, beams:2 * beams]
        out_ref[0, band, :] = (ded_re * ded_re + ded_im * ded_im) / channels


def dedisperse(kp1, dm_list, lags, spec, bins):
    sources, n_freq, _, chans, beams = spec.shape
    channels = sources * chans
    trials = dm_list.shape[0]
    resid = ((dm_list[:, None] * lags[None, :]) // 4096) % bins
    sample = jnp.arange(128, dtype=jnp.int32) % bins
    turns = (kp1[:, None] * sample[None, :]) % bins
    angles = turns.astype(jnp.float32) * (2.0 * math.pi / bins)
    tab = jnp.zeros((n_freq, 8, 128), jnp.float32)
    tab = tab.at[:, 0].set(jnp.cos(angles).astype(jnp.bfloat16).astype(jnp.float32))
    tab = tab.at[:, 1].set(jnp.sin(angles).astype(jnp.bfloat16).astype(jnp.float32))
    flops = 8 * n_freq * trials * channels * beams
    cost = pl.CostEstimate(
        flops=flops,
        transcendentals=0,
        bytes_accessed=trials * channels * 4 + n_freq * 2 * channels * beams * 2 + n_freq * trials * beams * 4,
    )
    return pl.pallas_call(
        partial(dedisp_kernel, channels=channels),
        out_shape=jax.ShapeDtypeStruct((n_freq, trials, beams), jnp.float32),
        grid=(n_freq,),
        in_specs=[
            pl.BlockSpec((trials, channels), lambda i: (0, 0)),
            pl.BlockSpec((1, 8, 128), lambda i: (i, 0, 0)),
            pl.BlockSpec((sources, 1, 2, chans, beams), lambda i: (0, i, 0, 0, 0)),
        ],
        out_specs=pl.BlockSpec((1, trials, beams), lambda i: (i, 0, 0)),
        scratch_shapes=[
            pltpu.VMEM((trials, 2 * channels), jnp.bfloat16),
            pltpu.VMEM((2 * channels, 2 * beams), jnp.bfloat16),
        ],
        compiler_params=pltpu.CompilerParams(vmem_limit_bytes=48 * 1024 * 1024),
        cost_estimate=cost,
    )(resid, tab, spec)


def beamform(volt_block, nu, beam_pos):
    n_chan, _, samples, antennas = volt_block.shape
    beams = beam_pos.shape[0]
    cos_w, sin_w = steering(nu, beam_pos, antennas)
    both = jnp.einsum(
        "cpsa,cab->cpsb", volt_block, jnp.concatenate([cos_w, sin_w], axis=2), preferred_element_type=jnp.float32
    )
    cosine_term = both[..., :beams]
    sin_part = both[..., beams:]
    real_part = cosine_term[:, 0] + sin_part[:, 1]
    imag_part = cosine_term[:, 1] - sin_part[:, 0]
    power_now = real_part * real_part + imag_part * imag_part
    return jnp.mean(power_now.reshape(n_chan, samples // 4, 4, beams), axis=2)


def spectra_of(history, fresh_bins):
    highest = lax.Precision.HIGHEST
    window = jnp.concatenate([history, fresh_bins], axis=1)
    bins = window.shape[1]
    scaled = window / (jnp.mean(window, axis=1, keepdims=True) + 1e-06)
    spectra = jnp.einsum("ctb,tj->jcb", scaled, dft_table(bins), precision=highest).astype(jnp.bfloat16)
    return spectra.reshape(bins // 2, 2, history.shape[0], history.shape[2])


def local(voltages, history, beam_pos, dm_list, chan_map):
    devices = lax.axis_size("gx")
    channel_count = devices * chan_map.shape[0]
    local_chan = voltages.shape[0]
    block_size = math.gcd(local_chan, 8)
    n_blocks = local_chan // block_size
    volt_blocks = voltages.reshape(n_blocks, block_size, *voltages.shape[1:])
    freq_blocks = (2 * channel_count - chan_map).reshape(n_blocks, block_size)
    slot = jnp.arange(channel_count, dtype=jnp.int32) // chan_map.shape[0]
    mine = jnp.where(slot == lax.axis_index("gx"), jnp.tile(chan_map, devices), 0)
    all_chan = lax.psum(mine, "gx")
    all_chan, volt_blocks = lax.optimization_barrier((all_chan, volt_blocks))
    fresh = [beamform(volt_blocks[i], freq_blocks[i], beam_pos) for i in range(n_blocks)]
    fresh_bins = jnp.concatenate(fresh, axis=0)
    spectra = spectra_of(history, fresh_bins)
    bins = 2 * spectra.shape[0]
    freq_dev = spectra.shape[0] // devices
    blocks = spectra.reshape(devices, freq_dev, *spectra.shape[1:])
    turned = lax.all_to_all(blocks, "gx", split_axis=0, concat_axis=0, tiled=True)
    lags = channel_lags(all_chan, channel_count)
    kp1 = lax.axis_index("gx") * freq_dev + jnp.arange(freq_dev, dtype=jnp.int32) + 1
    return dedisperse(kp1, dm_list, lags, turned, bins)


def solution(mesh):
    in_specs = (
        P(("groups", "gx"), None, None, None),
        P(("groups", "gx"), None, None),
        P(),
        P(),
        P("gx"),
    )
    out_specs = P(("groups", "gx"), None, None)
    return jax.shard_map(local, mesh=mesh, in_specs=in_specs, out_specs=out_specs, check_vma=False)
```

```python
from functools import partial
import math

import jax
import jax.numpy as jnp
from jax import lax
from jax.experimental import pallas as pl
from jax.experimental.pallas import tpu as pltpu
from jax.sharding import PartitionSpec as P

GRID = 32
PHASES = 8192


def axis_tables(nu, pos, scale):
    step = (nu[:, None] * pos[None, :]) % PHASES

    def trig(mult, factor):
        turns = (step[:, None, :] * (mult[None, :, None] * factor)) % PHASES
        angles = turns.astype(jnp.float32) * (2.0 * math.pi / PHASES)
        return jnp.cos(angles), jnp.sin(angles)

    lo = jnp.arange(8, dtype=jnp.int32)
    hi = jnp.arange(GRID // 8, dtype=jnp.int32)
    c_lo, s_lo = trig(lo, 1)
    c_hi, s_hi = trig(hi, 8)
    cos_t = c_hi[:, :, None, :] * c_lo[:, None, :, :] - s_hi[:, :, None, :] * s_lo[:, None, :, :]
    sin_t = s_hi[:, :, None, :] * c_lo[:, None, :, :] + c_hi[:, :, None, :] * s_lo[:, None, :, :]
    shape = (nu.shape[0], GRID, pos.shape[0])
    return cos_t.reshape(shape) * scale, sin_t.reshape(shape) * scale


def steering(nu, beam_pos, antennas):
    weight_scale = 1.0 / math.sqrt(antennas)
    ca, sa = axis_tables(nu, beam_pos[:, 0], weight_scale)
    cb, sb = axis_tables(nu, beam_pos[:, 1], 1.0)
    n_chan, _, beams = ca.shape
    w_cos = ca[:, None, :, :] * cb[:, :, None, :] - sa[:, None, :, :] * sb[:, :, None, :]
    w_sin = sa[:, None, :, :] * cb[:, :, None, :] + ca[:, None, :, :] * sb[:, :, None, :]
    w_cos = w_cos.reshape(n_chan, GRID * GRID, beams).astype(jnp.bfloat16)
    w_sin = w_sin.reshape(n_chan, GRID * GRID, beams).astype(jnp.bfloat16)
    return w_cos, w_sin


def dft_table(bins):
    sample = jnp.arange(bins, dtype=jnp.int32)
    harmonic = jnp.arange(bins // 2, dtype=jnp.int32) + 1
    turn_count = sample[:, None] * harmonic[None, :] % bins
    angles = turn_count.astype(jnp.float32) * (2.0 * math.pi / bins)
    norm_scale = 1.0 / math.sqrt(bins)
    both = jnp.stack([jnp.cos(angles) * norm_scale, -jnp.sin(angles) * norm_scale], axis=2)
    return both.reshape(bins, bins)


def channel_lags(chan_map, channel_count):
    freq_index = 2 * channel_count - chan_map
    top_square = 2 * channel_count * (2 * channel_count) * 64
    return top_square // (freq_index * freq_index) - 64


def dedisp_kernel(resid_ref, tab_ref, spec_ref, out_ref, lhs_buf, rhs_buf, *, channels):
    sources, _, _, chans, beams = spec_ref.shape
    for s in range(sources):
        s_re = spec_ref[s, 0, 0]
        s_im = spec_ref[s, 0, 1]
        lo, hi = s * chans, (s + 1) * chans
        rhs_buf[lo:hi, 0:beams] = s_re
        rhs_buf[lo:hi, beams:2 * beams] = s_im
        rhs_buf[channels + lo:channels + hi, 0:beams] = -s_im
        rhs_buf[channels + lo:channels + hi, beams:2 * beams] = s_re
    rows = resid_ref.shape[0]
    step = 64 if rows % 64 == 0 else rows
    cos_t = jnp.broadcast_to(tab_ref[0, 0:1, :], (step, 128))
    sin_t = jnp.broadcast_to(tab_ref[0, 1:2, :], (step, 128))
    for r in range(rows // step):
        band = slice(r * step, (r + 1) * step)
        for c in range(channels // 128):
            idx = resid_ref[band, c * 128:(c + 1) * 128]
            lhs_buf[band, c * 128:(c + 1) * 128] = jnp.take_along_axis(cos_t, idx, axis=1).astype(jnp.bfloat16)
            lhs_buf[band, channels + c * 128:channels + (c + 1) * 128] = (
                jnp.take_along_axis(sin_t, idx, axis=1).astype(jnp.bfloat16)
            )
        res = jnp.dot(lhs_buf[band, :], rhs_buf[...], preferred_element_type=jnp.float32)
        ded_re = res[:, 0:beams]
        ded_im = res[:, beams:2 * beams]
        out_ref[0, band, :] = (ded_re * ded_re + ded_im * ded_im) / channels


def dedisperse(kp1, dm_list, lags, spec, bins):
    sources, n_freq, _, chans, beams = spec.shape
    channels = sources * chans
    trials = dm_list.shape[0]
    resid = ((dm_list[:, None] * lags[None, :]) // 4096) % bins
    sample = jnp.arange(128, dtype=jnp.int32) % bins
    turns = (kp1[:, None] * sample[None, :]) % bins
    angles = turns.astype(jnp.float32) * (2.0 * math.pi / bins)
    tab = jnp.zeros((n_freq, 8, 128), jnp.float32)
    tab = tab.at[:, 0].set(jnp.cos(angles).astype(jnp.bfloat16).astype(jnp.float32))
    tab = tab.at[:, 1].set(jnp.sin(angles).astype(jnp.bfloat16).astype(jnp.float32))
    flops = 8 * n_freq * trials * channels * beams
    cost = pl.CostEstimate(
        flops=flops,
        transcendentals=0,
        bytes_accessed=trials * channels * 4 + n_freq * 2 * channels * beams * 2 + n_freq * trials * beams * 4,
    )
    return pl.pallas_call(
        partial(dedisp_kernel, channels=channels),
        out_shape=jax.ShapeDtypeStruct((n_freq, trials, beams), jnp.float32),
        grid=(n_freq,),
        in_specs=[
            pl.BlockSpec((trials, channels), lambda i: (0, 0)),
            pl.BlockSpec((1, 8, 128), lambda i: (i, 0, 0)),
            pl.BlockSpec((sources, 1, 2, chans, beams), lambda i: (0, i, 0, 0, 0)),
        ],
        out_specs=pl.BlockSpec((1, trials, beams), lambda i: (i, 0, 0)),
        scratch_shapes=[
            pltpu.VMEM((trials, 2 * channels), jnp.bfloat16),
            pltpu.VMEM((2 * channels, 2 * beams), jnp.bfloat16),
        ],
        compiler_params=pltpu.CompilerParams(vmem_limit_bytes=48 * 1024 * 1024),
        cost_estimate=cost,
    )(resid, tab, spec)


def beamform(volt_block, nu, beam_pos):
    n_chan, _, samples, antennas = volt_block.shape
    beams = beam_pos.shape[0]
    cos_w, sin_w = steering(nu, beam_pos, antennas)
    cosine_term = jnp.einsum("cpsa,cab->cpsb", volt_block, cos_w, preferred_element_type=jnp.float32)
    sin_part = jnp.einsum("cpsa,cab->cpsb", volt_block, sin_w, preferred_element_type=jnp.float32)
    real_part = cosine_term[:, 0] + sin_part[:, 1]
    imag_part = cosine_term[:, 1] - sin_part[:, 0]
    power_now = real_part * real_part + imag_part * imag_part
    return jnp.mean(power_now.reshape(n_chan, samples // 4, 4, beams), axis=2)


def spectra_of(history, fresh_bins):
    highest = lax.Precision.HIGHEST
    window = jnp.concatenate([history, fresh_bins], axis=1)
    bins = window.shape[1]
    scaled = window / (jnp.mean(window, axis=1, keepdims=True) + 1e-06)
    spectra = jnp.einsum("ctb,tj->jcb", scaled, dft_table(bins), precision=highest).astype(jnp.bfloat16)
    return spectra.reshape(bins // 2, 2, history.shape[0], history.shape[2])


def local(voltages, history, beam_pos, dm_list, chan_map):
    devices = lax.axis_size("gx")
    channel_count = devices * chan_map.shape[0]
    local_chan = voltages.shape[0]
    block_size = math.gcd(local_chan, 8)
    n_blocks = local_chan // block_size
    volt_blocks = voltages.reshape(n_blocks, block_size, *voltages.shape[1:])
    freq_blocks = (2 * channel_count - chan_map).reshape(n_blocks, block_size)
    slot = jnp.arange(channel_count, dtype=jnp.int32) // chan_map.shape[0]
    mine = jnp.where(slot == lax.axis_index("gx"), jnp.tile(chan_map, devices), 0)
    all_chan = lax.psum(mine, "gx")
    all_chan, volt_blocks = lax.optimization_barrier((all_chan, volt_blocks))
    fresh = [beamform(volt_blocks[i], freq_blocks[i], beam_pos) for i in range(n_blocks)]
    fresh_bins = jnp.concatenate(fresh, axis=0)
    spectra = spectra_of(history, fresh_bins)
    bins = 2 * spectra.shape[0]
    freq_dev = spectra.shape[0] // devices
    blocks = spectra.reshape(devices, freq_dev, *spectra.shape[1:])
    turned = lax.all_to_all(blocks, "gx", split_axis=0, concat_axis=0, tiled=True)
    lags = channel_lags(all_chan, channel_count)
    kp1 = lax.axis_index("gx") * freq_dev + jnp.arange(freq_dev, dtype=jnp.int32) + 1
    return dedisperse(kp1, dm_list, lags, turned, bins)


def solution(mesh):
    in_specs = (
        P(("groups", "gx"), None, None, None),
        P(("groups", "gx"), None, None),
        P(),
        P(),
        P("gx"),
    )
    out_specs = P(("groups", "gx"), None, None)
    return jax.shard_map(local, mesh=mesh, in_specs=in_specs, out_specs=out_specs, check_vma=False)
```
